32 devices in a mesh: groups: 2 (over y), expert: 16 (over z, x, core).
Axes of the slice: x: 2, y: 2, z: 4, core: 2. Of those that a mesh axis runs over, the one named last changes fastest.
Arguments:
- tokens: bfloat16 [128, 3072], P(('groups', 'expert')), parts along dimension 0, may hold values from -6 to 6
- cotangent: bfloat16 [128, 3072], P(('groups', 'expert')), parts along dimension 0, may hold values from -6 to 6
- expert_ids: int32 [128, 2], P(('groups', 'expert')), parts along dimension 0, may hold values from 0 to 7, all different within a row; in each aligned block of 4 rows (0 to 3, 4 to 7, ...) at most 2 rows name the same one
- gate_weights: bfloat16 [128, 2], P(('groups', 'expert')), parts along dimension 0, may hold values from 0.19921875 to 1
- w_gate: bfloat16 [65536, 3072], P('expert'), may hold values from -0.109375 to 0.109375
- w_up: bfloat16 [65536, 3072], P('expert'), may hold values from -0.109375 to 0.109375
- w_down: bfloat16 [65536, 3072], P('expert'), may hold values from -0.0625 to 0.0625
Outputs:
- layer_out: bfloat16 [128, 3072], P(('groups', 'expert')), parts along dimension 0
- input_grad: bfloat16 [128, 3072], P(('groups', 'expert')), parts along dimension 0
The draws below stay inside these ranges and needn't reach their ends.
There are 2 independent parts, one for each index of `groups`. The reference program is written for one: setup_inputs(seed, part) draws one part's arguments, and reference() takes and returns one part's arrays. A program takes and returns all parts, laid end to end along the dimension named above; an argument that names none is the same for every part. Nothing has to cross between parts.
Inputs may be any that keep to these rules, and one draw needn't show every extreme that they name: `expert_ids`: each token names two different experts. Among the 8 pairs of one device's tokens no expert is named more than 2 times, a bound that some block reaches.
All inputs are finite; a program needn't handle non-finite values.
Results may differ from the reference program's by a relative error of at most 0.0064.
Values may be sent and summed in bfloat16 or wider, within the bound.
No kernel may reach another device: no remote copies, remote signals or barrier semaphores. Data moves between devices by JAX's collectives and lax.ppermute only.
A program may use at most 192 MiB of HBM per device.

```python
import math
import jax
import jax.numpy as jnp
import numpy as np
from jax import lax

D = 3072
F = 8192
EXPERTS = 8
TOK_DEV = 4
CAP = 2
TOKENS = 64
N_EXPERT = 16


def block_scale(stream_key, extent, cuts, least, top_value):
    def one(axis_at, shards_of):
        heights = jax.random.uniform(jax.random.fold_in(jax.random.fold_in(stream_key, 6), axis_at), (shards_of,), jnp.float32, least / len(cuts), top_value / len(cuts))
        return jnp.repeat(jnp.exp(heights), extent[axis_at] // shards_of).reshape((-1,) + (1,) * (len(extent) - axis_at - 1))

    loudness = one(*cuts[0])
    for cut in cuts[1:]:
        loudness = loudness * one(*cut)
    return loudness


def shared_out(rng, own, number, rows, amount, top, bound, slope):
    ranking = jax.random.permutation(rng, amount)
    heavy_load, ordinary = load_shares(amount, rows * top, bound, slope, True), load_shares(amount, rows * top, bound, slope, False)
    places = jnp.arange(amount)

    def named(tallies, offset_by):
        used = int((tallies > 0).sum())
        fixed = max(1, used // 4)
        passed = fixed + (places - fixed + offset_by * (used - fixed)) % max(1, amount - fixed)
        return jnp.zeros((amount,), jnp.int32).at[ranking[jnp.where(places < fixed, places, passed)]].set(jnp.asarray(tallies, jnp.int32))

    tallies = jnp.where(number % 4 == 0, named(heavy_load, number // 4), named(ordinary, number - number // 4 - 1))
    mixed = jax.random.permutation(jax.random.fold_in(own, 3), amount)
    donor, sink = mixed[0:amount // 2 * 2:2], mixed[1:amount // 2 * 2:2]
    room = jnp.minimum(tallies[donor] - 1, bound - tallies[sink]) // 2
    room = jnp.where((donor == ranking[0]) | (sink == ranking[0]) | (tallies[sink] == 0), 0, jnp.maximum(room, 0))
    passed = jax.random.randint(jax.random.fold_in(own, 4), (amount // 2,), 0, 1 << 20) % (room + 1)
    tallies = tallies.at[donor].add(-passed).at[sink].add(passed)
    labels = jnp.searchsorted(jnp.cumsum(tallies), jnp.arange(rows * top), side="right").astype(jnp.int32)
    grid = labels.reshape(top, rows).T
    grid = grid[jax.random.permutation(jax.random.fold_in(own, 1), rows)]
    offset_by = jax.random.randint(jax.random.fold_in(own, 2), (rows, 1), 0, top)
    return jnp.take_along_axis(grid, (jnp.arange(top)[None, :] + offset_by) % top, axis=1)


def load_shares(amount, total, reach, slope, full):
    loads = [(1 << 20) // math.isqrt(standing ** slope) + 1 for standing in range(1, amount + 1)]
    largest = reach if full else min(reach, max(-(-total // amount), total * loads[0] // sum(loads)))
    least = 1 if total - largest >= amount - 1 else 0
    holding, rest = [largest] + [least] * (amount - 1), total - largest - least * (amount - 1)
    while rest > 0:
        free = [i for i in range(1, amount) if holding[i] < largest] or [i for i in range(1, amount) if holding[i] < reach]
        whole, remaining = sum([loads[i] for i in free]), rest
        for i in free:
            more = min(reach - holding[i], max(1, remaining * loads[i] // whole), rest)
            holding[i] = holding[i] + more
            rest = rest - more
    return np.array(holding)


def bell_draw(stream_key, dims, width, limit, shards=(), kind=jnp.bfloat16):
    array = width * jax.random.normal(stream_key, dims, jnp.float32)
    if shards:
        array = array * block_scale(stream_key, dims, shards, -0.22, 0.18)
    return jnp.clip(array, -limit, limit).astype(kind)


def setup_inputs(seed: int = 0, part: int = 0) -> dict:
    keys = jax.random.split(jax.random.key(seed), 8)
    part_splits = jax.random.split(jax.random.fold_in(keys[7], part), 8)
    tokens = bell_draw(part_splits[0], (TOKENS, D), 1.0, 6.0, ((0, 16),))
    cotangent = bell_draw(part_splits[1], (TOKENS, D), 1.0, 6.0, ((0, 16),))
    expert_ids_keys = jax.random.split(jax.random.fold_in(part_splits[2], 1), TOKENS // TOK_DEV)
    expert_ids_turns = jax.random.permutation(jax.random.fold_in(part_splits[2], 3), TOKENS // TOK_DEV)
    expert_ids = jax.vmap(lambda own, number: shared_out(jax.random.fold_in(part_splits[2], 2), own, number, TOK_DEV, EXPERTS, 2, CAP, 2))(expert_ids_keys, expert_ids_turns).reshape((TOKENS, 2))
    gate_weights = jnp.clip(0.19921875 + 0.80078125 * jax.random.uniform(part_splits[3], (TOKENS, 2), jnp.float32) ** block_scale(part_splits[3], (TOKENS, 2), ((0, 16),), -0.2, 0.2), 0.19921875, 1.0).astype(jnp.bfloat16)
    w_gate = bell_draw(keys[4], (EXPERTS * F, D), D ** -0.5, 0.109375, ((0, 16),))
    w_up = bell_draw(keys[5], (EXPERTS * F, D), D ** -0.5, 0.109375, ((0, 16),))
    w_down = bell_draw(keys[6], (EXPERTS * F, D), F ** -0.5, 0.0625, ((0, 16),))
    return dict(tokens=tokens, cotangent=cotangent, expert_ids=expert_ids, gate_weights=gate_weights, w_gate=w_gate, w_up=w_up, w_down=w_down)


def slot_ranks(routes):
    count = routes.shape[-1]
    order = jnp.arange(count, dtype=jnp.int32)
    earlier = order[None, :] < order[:, None]
    same = routes[..., :, None] == routes[..., None, :]
    return jnp.sum(jnp.logical_and(same, earlier), axis=-1).astype(jnp.int32)


def owner_work(token_rows, cotan_rows, gate_rows, up_rows, down_rows):
    gate_proj = jnp.dot(token_rows, gate_rows.T, preferred_element_type=jnp.float32)
    up_proj = jnp.dot(token_rows, up_rows.T, preferred_element_type=jnp.float32)
    sigmoid = jax.nn.sigmoid(gate_proj)
    activated = gate_proj * sigmoid
    hidden = (activated * up_proj).astype(jnp.bfloat16)
    out_part = jnp.dot(hidden, down_rows, preferred_element_type=jnp.float32).astype(jnp.bfloat16)
    hidden_grad = jnp.dot(cotan_rows, down_rows.T, preferred_element_type=jnp.float32)
    gate_grad = (hidden_grad * up_proj * sigmoid * (1.0 + gate_proj * (1.0 - sigmoid))).astype(jnp.bfloat16)
    up_grad = (hidden_grad * activated).astype(jnp.bfloat16)
    grad_part = jnp.dot(gate_grad, gate_rows, preferred_element_type=jnp.float32)
    grad_part = grad_part + jnp.dot(up_grad, up_rows, preferred_element_type=jnp.float32)
    return out_part, grad_part.astype(jnp.bfloat16)


def reference(tokens, cotangent, expert_ids, gate_weights, w_gate, w_up, w_down):
    owner_count = N_EXPERT // EXPERTS
    share = F // owner_count
    pair_count = TOK_DEV * 2
    routes = expert_ids.reshape(N_EXPERT, pair_count)
    rank_index = slot_ranks(routes)
    slot_index = (routes * CAP + rank_index).astype(jnp.int32)
    source = jnp.arange(N_EXPERT, dtype=jnp.int32)[:, None]
    token_pairs = jnp.repeat(tokens, 2, axis=0).reshape(N_EXPERT, pair_count, D)
    scaled = (gate_weights.reshape(-1, 1).astype(jnp.float32) * jnp.repeat(cotangent, 2, axis=0).astype(jnp.float32)).astype(jnp.bfloat16)
    scaled = scaled.reshape(N_EXPERT, pair_count, D)
    token_slots = jnp.zeros((N_EXPERT, EXPERTS * CAP, D), jnp.bfloat16).at[source, slot_index].set(token_pairs)
    cotan_slots = jnp.zeros((N_EXPERT, EXPERTS * CAP, D), jnp.bfloat16).at[source, slot_index].set(scaled)
    token_slots = token_slots.reshape(N_EXPERT, EXPERTS, CAP, D).transpose(1, 0, 2, 3).reshape(EXPERTS, N_EXPERT * CAP, D)
    cotan_slots = cotan_slots.reshape(N_EXPERT, EXPERTS, CAP, D).transpose(1, 0, 2, 3).reshape(EXPERTS, N_EXPERT * CAP, D)
    gate_all = w_gate.reshape(EXPERTS, owner_count, share, D)
    up_all = w_up.reshape(EXPERTS, owner_count, share, D)
    down_all = w_down.reshape(EXPERTS, owner_count, share, D)

    def expert_step(unused, inputs):
        token_rows, cotan_rows, gate_set, up_set, down_set = inputs

        def owner_step(carry, weights):
            out_sum, grad_sum = carry
            out_part, grad_part = owner_work(token_rows, cotan_rows, weights[0], weights[1], weights[2])
            return (out_sum + out_part.astype(jnp.float32), grad_sum + grad_part.astype(jnp.float32)), None

        start = jnp.zeros((N_EXPERT * CAP, D), jnp.float32)
        sums, unused_out = lax.scan(owner_step, (start, start), (gate_set, up_set, down_set))
        return unused, sums

    unused, sums = lax.scan(expert_step, 0, (token_slots, cotan_slots, gate_all, up_all, down_all))
    out_sum = sums[0].reshape(EXPERTS, N_EXPERT, CAP, D)
    grad_sum = sums[1].reshape(EXPERTS, N_EXPERT, CAP, D)
    picked_out = out_sum[routes, source, rank_index].reshape(TOKENS, 2, D)
    picked_grad = grad_sum[routes, source, rank_index].reshape(TOKENS, 2, D)
    layer_out = jnp.sum(picked_out * gate_weights.astype(jnp.float32)[:, :, None], axis=1).astype(jnp.bfloat16)
    input_grad = jnp.sum(picked_grad, axis=1).astype(jnp.bfloat16)
    return layer_out, input_grad
```

```python
import functools

import jax
import jax.numpy as jnp
from jax import lax
from jax.experimental import pallas as pl
from jax.experimental.pallas import tpu as pltpu
from jax.sharding import PartitionSpec as P

EXPERTS = 8
CAP = 2
NT = (((1,), (1,)), ((), ()))


def slot_ranks(routes):
    count = routes.shape[-1]
    order = jnp.arange(count, dtype=jnp.int32)
    earlier = order[None, :] < order[:, None]
    same = routes[..., :, None] == routes[..., None, :]
    return jnp.sum(jnp.logical_and(same, earlier), axis=-1)


def expert_kernel(x_ref, c_ref, wg_ref, wu_ref, wd_ref, out_ref, grad_ref, acc_out, acc_grad):
    step = pl.program_id(0)

    @pl.when(step == 0)
    def _():
        acc_out[...] = jnp.zeros_like(acc_out)
        acc_grad[...] = jnp.zeros_like(acc_grad)

    x = x_ref[...]
    c = c_ref[...]
    wg = wg_ref[...]
    wu = wu_ref[...]
    wd = wd_ref[...]
    gate_proj = lax.dot_general(x, wg, NT, preferred_element_type=jnp.float32)
    up_proj = lax.dot_general(x, wu, NT, preferred_element_type=jnp.float32)
    sigmoid = jax.nn.sigmoid(gate_proj)
    activated = gate_proj * sigmoid
    hidden = (activated * up_proj).astype(jnp.bfloat16)
    acc_out[...] += jnp.dot(hidden, wd, preferred_element_type=jnp.float32)
    hidden_grad = lax.dot_general(c, wd, NT, preferred_element_type=jnp.float32)
    gate_grad = (hidden_grad * up_proj * sigmoid * (1.0 + gate_proj * (1.0 - sigmoid))).astype(
        jnp.bfloat16
    )
    up_grad = (hidden_grad * activated).astype(jnp.bfloat16)
    acc_grad[...] += jnp.dot(gate_grad, wg, preferred_element_type=jnp.float32) + jnp.dot(
        up_grad, wu, preferred_element_type=jnp.float32
    )

    @pl.when(step == pl.num_programs(0) - 1)
    def _():
        out_ref[...] = acc_out[...].astype(out_ref.dtype)
        grad_ref[...] = acc_grad[...].astype(grad_ref.dtype)


def expert_work(rows, w_gate, w_up, w_down):
    m = rows.shape[0]
    hidden_units, features = w_gate.shape
    block = min(512, hidden_units)
    steps = hidden_units // block
    row_spec = lambda half: pl.BlockSpec((m, features), lambda i: (0, half))
    w_spec = pl.BlockSpec((block, features), lambda i: (i, 0))
    out_spec = pl.BlockSpec((m, features), lambda i: (0, 0))
    cost = pl.CostEstimate(
        flops=12 * m * hidden_units * features,
        transcendentals=m * hidden_units,
        bytes_accessed=3 * hidden_units * features * 2 + 4 * m * features * 2,
    )
    return pl.pallas_call(
        expert_kernel,
        grid=(steps,),
        in_specs=[row_spec(0), row_spec(1), w_spec, w_spec, w_spec],
        out_specs=[out_spec, out_spec],
        out_shape=[jax.ShapeDtypeStruct((m, features), jnp.bfloat16)] * 2,
        scratch_shapes=[pltpu.VMEM((m, features), jnp.float32)] * 2,
        compiler_params=pltpu.CompilerParams(
            dimension_semantics=("arbitrary",), vmem_limit_bytes=48 * 1024 * 1024
        ),
        cost_estimate=cost,
    )(rows, rows, w_gate, w_up, w_down)


def shards(tokens, cotangent, expert_ids, gate_weights, w_gate, w_up, w_down):
    devices = lax.axis_size("expert")
    owner_count = devices // EXPERTS
    tok_count = tokens.shape[0]
    features = tokens.shape[1]
    pair_count = tok_count * 2
    routes = expert_ids.reshape(pair_count)
    rank_index = slot_ranks(routes)
    slot_index = routes * CAP + rank_index
    token_pairs = jnp.repeat(tokens, 2, axis=0)
    scaled = (
        gate_weights.reshape(pair_count, 1).astype(jnp.float32)
        * jnp.repeat(cotangent, 2, axis=0).astype(jnp.float32)
    ).astype(jnp.bfloat16)
    both = jnp.concatenate([token_pairs, scaled], axis=1)
    slots = jnp.zeros((EXPERTS * CAP, 2 * features), jnp.bfloat16).at[slot_index].set(both)
    send = jnp.repeat(slots.reshape(EXPERTS, CAP, 2 * features), owner_count, axis=0)
    recv = lax.all_to_all(send, "expert", split_axis=0, concat_axis=0, tiled=True)
    shape = (devices, CAP, features)
    out_part, grad_part = expert_work(recv.reshape(-1, 2 * features), w_gate, w_up, w_down)
    back = jnp.concatenate([out_part.reshape(shape), grad_part.reshape(shape)], axis=2)
    home = lax.all_to_all(back, "expert", split_axis=0, concat_axis=0, tiled=True)
    sums = jnp.sum(
        home.reshape(EXPERTS, owner_count, CAP, 2 * features).astype(jnp.float32), axis=1
    ).reshape(EXPERTS * CAP, 2 * features)
    picked = sums[slot_index].reshape(tok_count, 2, 2 * features)
    picked_out = picked[:, :, :features]
    picked_grad = picked[:, :, features:]
    layer_out = jnp.sum(picked_out * gate_weights.astype(jnp.float32)[:, :, None], axis=1).astype(
        jnp.bfloat16
    )
    input_grad = jnp.sum(picked_grad, axis=1).astype(jnp.bfloat16)
    return (layer_out, input_grad)


def solution(mesh):
    in_specs = (
        P(("groups", "expert"), None),
        P(("groups", "expert"), None),
        P(("groups", "expert"), None),
        P(("groups", "expert"), None),
        P("expert", None),
        P("expert", None),
        P("expert", None),
    )
    out_specs = (P(("groups", "expert"), None), P(("groups", "expert"), None))
    return jax.shard_map(shards, mesh=mesh, in_specs=in_specs, out_specs=out_specs, check_vma=False)
```

```python
import functools

import jax
import jax.numpy as jnp
from jax import lax
from jax.experimental import pallas as pl
from jax.experimental.pallas import tpu as pltpu
from jax.sharding import PartitionSpec as P

EXPERTS = 8
CAP = 2
NT = (((1,), (1,)), ((), ()))


def slot_ranks(routes):
    count = routes.shape[-1]
    order = jnp.arange(count, dtype=jnp.int32)
    earlier = order[None, :] < order[:, None]
    same = routes[..., :, None] == routes[..., None, :]
    return jnp.sum(jnp.logical_and(same, earlier), axis=-1)


def expert_kernel(offset_ref, x_ref, c_ref, wg_ref, wu_ref, wd_ref, out_ref, acc_out, acc_grad):
    step = pl.program_id(0)
    features = acc_out.shape[1]

    @pl.when(step == 0)
    def _():
        acc_out[...] = jnp.zeros_like(acc_out)
        acc_grad[...] = jnp.zeros_like(acc_grad)

    x = x_ref[...]
    c = c_ref[...]
    wg = wg_ref[...]
    wu = wu_ref[...]
    wd = wd_ref[...]
    gate_proj = lax.dot_general(x, wg, NT, preferred_element_type=jnp.float32)
    up_proj = lax.dot_general(x, wu, NT, preferred_element_type=jnp.float32)
    sigmoid = jax.nn.sigmoid(gate_proj)
    activated = gate_proj * sigmoid
    hidden = (activated * up_proj).astype(jnp.bfloat16)
    acc_out[...] += jnp.dot(hidden, wd, preferred_element_type=jnp.float32)
    hidden_grad = lax.dot_general(c, wd, NT, preferred_element_type=jnp.float32)
    gate_grad = (hidden_grad * up_proj * sigmoid * (1.0 + gate_proj * (1.0 - sigmoid))).astype(
        jnp.bfloat16
    )
    up_grad = (hidden_grad * activated).astype(jnp.bfloat16)
    acc_grad[...] += jnp.dot(gate_grad, wg, preferred_element_type=jnp.float32) + jnp.dot(
        up_grad, wu, preferred_element_type=jnp.float32
    )

    @pl.when(step == pl.num_programs(0) - 1)
    def _():
        out_ref[:, :features] = acc_out[...].astype(out_ref.dtype)
        out_ref[:, features:] = acc_grad[...].astype(out_ref.dtype)


def expert_work(rows, w_gate, w_up, w_down, part, parts):
    m = rows.shape[0]
    hidden_units, features = w_gate.shape
    share = hidden_units // parts
    block = min(256, share)
    steps = share // block
    offset = jnp.reshape(part * steps, (1,)).astype(jnp.int32)
    row_spec = lambda half: pl.BlockSpec((m, features), lambda i, off: (0, half))
    w_spec = pl.BlockSpec((block, features), lambda i, off: (off[0] + i, 0))
    out_spec = pl.BlockSpec((m, 2 * features), lambda i, off: (0, 0))
    cost = pl.CostEstimate(
        flops=12 * m * share * features,
        transcendentals=m * share,
        bytes_accessed=3 * share * features * 2 + 4 * m * features * 2,
    )
    grid_spec = pltpu.PrefetchScalarGridSpec(
        num_scalar_prefetch=1,
        grid=(steps,),
        in_specs=[row_spec(0), row_spec(1), w_spec, w_spec, w_spec],
        out_specs=out_spec,
        scratch_shapes=[pltpu.VMEM((m, features), jnp.float32)] * 2,
    )
    return pl.pallas_call(
        expert_kernel,
        grid_spec=grid_spec,
        out_shape=jax.ShapeDtypeStruct((m, 2 * features), jnp.bfloat16),
        compiler_params=pltpu.CompilerParams(
            dimension_semantics=("arbitrary",), vmem_limit_bytes=48 * 1024 * 1024
        ),
        cost_estimate=cost,
    )(offset, rows, rows, w_gate, w_up, w_down)


def shards(tokens, cotangent, expert_ids, gate_weights, w_gate, w_up, w_down):
    devices = lax.axis_size("expert")
    parts = lax.axis_size("groups")
    part = lax.axis_index("groups")
    owner_count = devices // EXPERTS
    tok_count = tokens.shape[0]
    features = tokens.shape[1]
    pair_count = tok_count * 2
    routes = expert_ids.reshape(pair_count)
    rank_index = slot_ranks(routes)
    slot_index = routes * CAP + rank_index
    token_pairs = jnp.repeat(tokens, 2, axis=0)
    scaled = (
        gate_weights.reshape(pair_count, 1).astype(jnp.float32)
        * jnp.repeat(cotangent, 2, axis=0).astype(jnp.float32)
    ).astype(jnp.bfloat16)
    both = jnp.concatenate([token_pairs, scaled], axis=1)
    slots = jnp.zeros((EXPERTS * CAP, 2 * features), jnp.bfloat16).at[slot_index].set(both)
    send = jnp.repeat(slots.reshape(EXPERTS, CAP, 2 * features), owner_count, axis=0)
    send = jnp.tile(send, (parts, 1, 1))
    axes = ("groups", "expert")
    recv = lax.all_to_all(send, axes, split_axis=0, concat_axis=0, tiled=True)
    partials = expert_work(recv.reshape(-1, 2 * features), w_gate, w_up, w_down, part, parts)
    back = partials.reshape(parts * devices, CAP, 2 * features)
    home = lax.all_to_all(back, axes, split_axis=0, concat_axis=0, tiled=True)
    sums = jnp.sum(
        home.reshape(parts, EXPERTS, owner_count, CAP, 2 * features).astype(jnp.float32),
        axis=(0, 2),
    ).reshape(EXPERTS * CAP, 2 * features)
    picked = sums[slot_index].reshape(tok_count, 2, 2 * features)
    picked_out = picked[:, :, :features]
    picked_grad = picked[:, :, features:]
    layer_out = jnp.sum(picked_out * gate_weights.astype(jnp.float32)[:, :, None], axis=1).astype(
        jnp.bfloat16
    )
    input_grad = jnp.sum(picked_grad, axis=1).astype(jnp.bfloat16)
    return (layer_out, input_grad)


def solution(mesh):
    in_specs = (
        P(("groups", "expert"), None),
        P(("groups", "expert"), None),
        P(("groups", "expert"), None),
        P(("groups", "expert"), None),
        P("expert", None),
        P("expert", None),
        P("expert", None),
    )
    out_specs = (P(("groups", "expert"), None), P(("groups", "expert"), None))
    return jax.shard_map(shards, mesh=mesh, in_specs=in_specs, out_specs=out_specs, check_vma=False)
```

```python
import functools

import jax
import jax.numpy as jnp
from jax import lax
from jax.experimental import pallas as pl
from jax.experimental.pallas import tpu as pltpu
from jax.sharding import PartitionSpec as P

EXPERTS = 8
CAP = 2
NT = (((1,), (1,)), ((), ()))


def slot_ranks(routes):
    count = routes.shape[-1]
    order = jnp.arange(count, dtype=jnp.int32)
    earlier = order[None, :] < order[:, None]
    same = routes[..., :, None] == routes[..., None, :]
    return jnp.sum(jnp.logical_and(same, earlier), axis=-1)


def expert_kernel(offset_ref, x_ref, c_ref, wg_ref, wu_ref, wd_ref, out_ref, acc_out, acc_grad):
    step = pl.program_id(0)
    features = acc_out.shape[1]

    @pl.when(step == 0)
    def _():
        acc_out[...] = jnp.zeros_like(acc_out)
        acc_grad[...] = jnp.zeros_like(acc_grad)

    x = x_ref[...]
    c = c_ref[...]
    wg = wg_ref[...]
    wu = wu_ref[...]
    wd = wd_ref[...]
    gate_proj = lax.dot_general(x, wg, NT, preferred_element_type=jnp.float32)
    up_proj = lax.dot_general(x, wu, NT, preferred_element_type=jnp.float32)
    sigmoid = jax.nn.sigmoid(gate_proj)
    activated = gate_proj * sigmoid
    hidden = (activated * up_proj).astype(jnp.bfloat16)
    acc_out[...] += jnp.dot(hidden, wd, preferred_element_type=jnp.float32)
    hidden_grad = lax.dot_general(c, wd, NT, preferred_element_type=jnp.float32)
    gate_grad = (hidden_grad * up_proj * sigmoid * (1.0 + gate_proj * (1.0 - sigmoid))).astype(
        jnp.bfloat16
    )
    up_grad = (hidden_grad * activated).astype(jnp.bfloat16)
    acc_grad[...] += jnp.dot(gate_grad, wg, preferred_element_type=jnp.float32) + jnp.dot(
        up_grad, wu, preferred_element_type=jnp.float32
    )

    @pl.when(step == pl.num_programs(0) - 1)
    def _():
        out_ref[:, :features] = acc_out[...].astype(out_ref.dtype)
        out_ref[:, features:] = acc_grad[...].astype(out_ref.dtype)


def expert_work(rows, w_gate, w_up, w_down, part, parts):
    m = rows.shape[0]
    hidden_units, features = w_gate.shape
    share = hidden_units // parts
    block = min(512, share)
    steps = share // block
    offset = jnp.reshape(part * steps, (1,)).astype(jnp.int32)
    row_spec = lambda half: pl.BlockSpec((m, features), lambda i, off: (0, half))
    w_spec = pl.BlockSpec((block, features), lambda i, off: (off[0] + i, 0))
    out_spec = pl.BlockSpec((m, 2 * features), lambda i, off: (0, 0))
    cost = pl.CostEstimate(
        flops=12 * m * share * features,
        transcendentals=m * share,
        bytes_accessed=3 * share * features * 2 + 4 * m * features * 2,
    )
    grid_spec = pltpu.PrefetchScalarGridSpec(
        num_scalar_prefetch=1,
        grid=(steps,),
        in_specs=[row_spec(0), row_spec(1), w_spec, w_spec, w_spec],
        out_specs=out_spec,
        scratch_shapes=[pltpu.VMEM((m, features), jnp.float32)] * 2,
    )
    return pl.pallas_call(
        expert_kernel,
        grid_spec=grid_spec,
        out_shape=jax.ShapeDtypeStruct((m, 2 * features), jnp.bfloat16),
        compiler_params=pltpu.CompilerParams(
            dimension_semantics=("arbitrary",), vmem_limit_bytes=48 * 1024 * 1024
        ),
        cost_estimate=cost,
    )(offset, rows, rows, w_gate, w_up, w_down)


def shards(tokens, cotangent, expert_ids, gate_weights, w_gate, w_up, w_down):
    devices = lax.axis_size("expert")
    owner_count = devices // EXPERTS
    tok_count = tokens.shape[0]
    features = tokens.shape[1]
    pair_count = tok_count * 2
    routes = expert_ids.reshape(pair_count)
    rank_index = slot_ranks(routes)
    slot_index = routes * CAP + rank_index
    row_slot = (jnp.arange(devices * CAP) // (CAP * owner_count)) * CAP + jnp.arange(devices * CAP) % CAP
    hit = (row_slot[:, None] == slot_index[None, :]).reshape(devices * CAP, tok_count, 2)
    pick_tok = jnp.sum(hit, axis=2).astype(jnp.bfloat16)
    pick_cot = jnp.sum(jnp.where(hit, gate_weights[None, :, :], 0), axis=2).astype(jnp.bfloat16)
    send_tok = jnp.dot(pick_tok, tokens, preferred_element_type=jnp.float32)
    send_cot = jnp.dot(pick_cot, cotangent, preferred_element_type=jnp.float32)
    send = jnp.concatenate([send_tok, send_cot], axis=1).astype(jnp.bfloat16)
    send = send.reshape(devices, CAP, 2 * features)
    recv = lax.all_to_all(send, "expert", split_axis=0, concat_axis=0, tiled=True)
    partials = expert_work(recv.reshape(-1, 2 * features), w_gate, w_up, w_down, 0, 1)
    back = partials.reshape(devices, CAP, 2 * features)
    home = lax.all_to_all(back, "expert", split_axis=0, concat_axis=0, tiled=True)
    home = home.reshape(devices * CAP, 2 * features)
    take = jnp.transpose(hit, (1, 2, 0))
    take_out = jnp.sum(jnp.where(take, gate_weights[:, :, None], 0), axis=1).astype(jnp.bfloat16)
    take_grad = jnp.sum(take, axis=1).astype(jnp.bfloat16)
    layer_out = jnp.dot(take_out, home[:, :features], preferred_element_type=jnp.float32)
    input_grad = jnp.dot(take_grad, home[:, features:], preferred_element_type=jnp.float32)
    return (layer_out.astype(jnp.bfloat16), input_grad.astype(jnp.bfloat16))


def solution(mesh):
    in_specs = (
        P(("groups", "expert"), None),
        P(("groups", "expert"), None),
        P(("groups", "expert"), None),
        P(("groups", "expert"), None),
        P("expert", None),
        P("expert", None),
        P("expert", None),
    )
    out_specs = (P(("groups", "expert"), None), P(("groups", "expert"), None))
    return jax.shard_map(shards, mesh=mesh, in_specs=in_specs, out_specs=out_specs, check_vma=False)
```

```python
import functools

import jax
import jax.numpy as jnp
from jax import lax
from jax.experimental import pallas as pl
from jax.experimental.pallas import tpu as pltpu
from jax.sharding import PartitionSpec as P

EXPERTS = 8
CAP = 2
NT = (((1,), (1,)), ((), ()))


def slot_ranks(routes):
    count = routes.shape[-1]
    order = jnp.arange(count, dtype=jnp.int32)
    earlier = order[None, :] < order[:, None]
    same = routes[..., :, None] == routes[..., None, :]
    return jnp.sum(jnp.logical_and(same, earlier), axis=-1)


def expert_kernel(offset_ref, x_ref, c_ref, wg_ref, wu_ref, wd_ref, out_ref, acc_out, acc_grad):
    step = pl.program_id(0)
    features = acc_out.shape[1]

    @pl.when(step == 0)
    def _():
        acc_out[...] = jnp.zeros_like(acc_out)
        acc_grad[...] = jnp.zeros_like(acc_grad)

    m = acc_out.shape[0]
    x = x_ref[...].reshape(m, features)
    c = c_ref[...].reshape(m, features)
    wg = wg_ref[...]
    wu = wu_ref[...]
    wd = wd_ref[...]
    gate_proj = lax.dot_general(x, wg, NT, preferred_element_type=jnp.float32)
    up_proj = lax.dot_general(x, wu, NT, preferred_element_type=jnp.float32)
    sigmoid = jax.nn.sigmoid(gate_proj)
    activated = gate_proj * sigmoid
    hidden = (activated * up_proj).astype(jnp.bfloat16)
    acc_out[...] += jnp.dot(hidden, wd, preferred_element_type=jnp.float32)
    hidden_grad = lax.dot_general(c, wd, NT, preferred_element_type=jnp.float32)
    gate_grad = (hidden_grad * up_proj * sigmoid * (1.0 + gate_proj * (1.0 - sigmoid))).astype(
        jnp.bfloat16
    )
    up_grad = (hidden_grad * activated).astype(jnp.bfloat16)
    acc_grad[...] += jnp.dot(gate_grad, wg, preferred_element_type=jnp.float32) + jnp.dot(
        up_grad, wu, preferred_element_type=jnp.float32
    )

    @pl.when(step == pl.num_programs(0) - 1)
    def _():
        rows = out_ref.shape[:2]
        out_ref[:, :, :features] = acc_out[...].astype(out_ref.dtype).reshape(rows + (features,))
        out_ref[:, :, features:] = acc_grad[...].astype(out_ref.dtype).reshape(rows + (features,))


def expert_work(rows, w_gate, w_up, w_down, part, parts):
    chunks, cap = rows.shape[:2]
    m = chunks * cap
    hidden_units, features = w_gate.shape
    share = hidden_units // parts
    block = min(512, share)
    steps = share // block
    offset = jnp.reshape(part * steps, (1,)).astype(jnp.int32)
    row_spec = lambda half: pl.BlockSpec((chunks, cap, features), lambda i, off: (0, 0, half))
    w_spec = pl.BlockSpec((block, features), lambda i, off: (off[0] + i, 0))
    out_spec = pl.BlockSpec((chunks, cap, 2 * features), lambda i, off: (0, 0, 0))
    cost = pl.CostEstimate(
        flops=12 * m * share * features,
        transcendentals=m * share,
        bytes_accessed=3 * share * features * 2 + 4 * m * features * 2,
    )
    grid_spec = pltpu.PrefetchScalarGridSpec(
        num_scalar_prefetch=1,
        grid=(steps,),
        in_specs=[row_spec(0), row_spec(1), w_spec, w_spec, w_spec],
        out_specs=out_spec,
        scratch_shapes=[pltpu.VMEM((m, features), jnp.float32)] * 2,
    )
    return pl.pallas_call(
        expert_kernel,
        grid_spec=grid_spec,
        out_shape=jax.ShapeDtypeStruct((chunks, cap, 2 * features), jnp.bfloat16),
        compiler_params=pltpu.CompilerParams(
            dimension_semantics=("arbitrary",), vmem_limit_bytes=48 * 1024 * 1024
        ),
        cost_estimate=cost,
    )(offset, rows, rows, w_gate, w_up, w_down)


def pack_kernel(owner_count, ids_ref, gw_ref, tok_ref, cot_ref, out_ref):
    features = tok_ref.shape[1]
    pairs = ids_ref.shape[0]
    out_ref[...] = jnp.zeros_like(out_ref)
    for p in range(pairs):
        e = ids_ref[p]
        rank = jnp.int32(0)
        for q in range(p):
            rank = rank + (ids_ref[q] == e).astype(jnp.int32)
        t = p // 2
        tok_row = tok_ref[t:t + 1, :]
        cot_row = (gw_ref[p] * cot_ref[t:t + 1, :].astype(jnp.float32)).astype(out_ref.dtype)
        for j in range(owner_count):
            o = e * owner_count + j
            for r in range(CAP):
                keep = rank == r
                out_ref[o, r:r + 1, :features] = jnp.where(keep, tok_row, out_ref[o, r:r + 1, :features])
                out_ref[o, r:r + 1, features:] = jnp.where(keep, cot_row, out_ref[o, r:r + 1, features:])

def unpack_kernel(owner_count, ids_ref, gw_ref, home_ref, out_ref, grad_ref):
    features = out_ref.shape[1]
    pairs = ids_ref.shape[0]
    for t in range(pairs // 2):
        total_out = jnp.zeros((1, features), jnp.float32)
        total_grad = jnp.zeros((1, features), jnp.float32)
        for k in range(2):
            p = 2 * t + k
            e = ids_ref[p]
            rank = jnp.int32(0)
            for q in range(p):
                rank = rank + (ids_ref[q] == e).astype(jnp.int32)
            part_out = jnp.zeros((1, features), jnp.float32)
            part_grad = jnp.zeros((1, features), jnp.float32)
            for j in range(owner_count):
                block = home_ref[e * owner_count + j].astype(jnp.float32)
                row = jnp.where(rank == 0, block[0:1], block[1:2])
                part_out = part_out + row[:, :features]
                part_grad = part_grad + row[:, features:]
            total_out = total_out + gw_ref[p] * part_out
            total_grad = total_grad + part_grad
        out_ref[t:t + 1, :] = total_out.astype(out_ref.dtype)
        grad_ref[t:t + 1, :] = total_grad.astype(grad_ref.dtype)

SMEM_SPEC = pl.BlockSpec(memory_space=pltpu.SMEM)
VMEM_SPEC = pl.BlockSpec(memory_space=pltpu.VMEM)

def pack(tokens, cotangent, expert_ids, gate_weights, devices):
    owner_count = devices // EXPERTS
    tok_count, features = tokens.shape
    ids = expert_ids.reshape(-1).astype(jnp.int32)
    gw = gate_weights.reshape(-1).astype(jnp.float32)
    return pl.pallas_call(
        functools.partial(pack_kernel, owner_count),
        in_specs=[SMEM_SPEC, SMEM_SPEC, VMEM_SPEC, VMEM_SPEC],
        out_specs=VMEM_SPEC,
        out_shape=jax.ShapeDtypeStruct((devices, CAP, 2 * features), tokens.dtype),
    )(ids, gw, tokens, cotangent)

def unpack(home, expert_ids, gate_weights, devices):
    owner_count = devices // EXPERTS
    tok_count = expert_ids.shape[0]
    features = home.shape[2] // 2
    ids = expert_ids.reshape(-1).astype(jnp.int32)
    gw = gate_weights.reshape(-1).astype(jnp.float32)
    return pl.pallas_call(
        functools.partial(unpack_kernel, owner_count),
        in_specs=[SMEM_SPEC, SMEM_SPEC, VMEM_SPEC],
        out_specs=[VMEM_SPEC, VMEM_SPEC],
        out_shape=[jax.ShapeDtypeStruct((tok_count, features), home.dtype)] * 2,
    )(ids, gw, home)


def shards(tokens, cotangent, expert_ids, gate_weights, w_gate, w_up, w_down):
    devices = lax.axis_size("expert")
    send = pack(tokens, cotangent, expert_ids, gate_weights, devices)
    recv = lax.all_to_all(send, "expert", split_axis=0, concat_axis=0, tiled=True)
    partials = expert_work(recv, w_gate, w_up, w_down, 0, 1)
    home = lax.all_to_all(partials, "expert", split_axis=0, concat_axis=0, tiled=True)
    layer_out, input_grad = unpack(home, expert_ids, gate_weights, devices)
    return (layer_out, input_grad)


def solution(mesh):
    in_specs = (
        P(("groups", "expert"), None),
        P(("groups", "expert"), None),
        P(("groups", "expert"), None),
        P(("groups", "expert"), None),
        P("expert", None),
        P("expert", None),
        P("expert", None),
    )
    out_specs = (P(("groups", "expert"), None), P(("groups", "expert"), None))
    return jax.shard_map(shards, mesh=mesh, in_specs=in_specs, out_specs=out_specs, check_vma=False)
```

```python
import functools

import jax
import jax.numpy as jnp
from jax import lax
from jax.experimental import pallas as pl
from jax.experimental.pallas import tpu as pltpu
from jax.sharding import PartitionSpec as P

EXPERTS = 8
CAP = 2
NT = (((1,), (1,)), ((), ()))


def slot_ranks(routes):
    count = routes.shape[-1]
    order = jnp.arange(count, dtype=jnp.int32)
    earlier = order[None, :] < order[:, None]
    same = routes[..., :, None] == routes[..., None, :]
    return jnp.sum(jnp.logical_and(same, earlier), axis=-1)


def expert_kernel(offset_ref, x_ref, c_ref, wg_ref, wu_ref, wd_ref, out_ref, acc_out, acc_grad):
    step = pl.program_id(0)
    features = acc_out.shape[1]

    @pl.when(step == 0)
    def _():
        acc_out[...] = jnp.zeros_like(acc_out)
        acc_grad[...] = jnp.zeros_like(acc_grad)

    m = acc_out.shape[0]
    x = x_ref[...].reshape(m, features)
    c = c_ref[...].reshape(m, features)
    wg = wg_ref[...]
    wu = wu_ref[...]
    wd = wd_ref[...]
    gate_proj = lax.dot_general(x, wg, NT, preferred_element_type=jnp.float32)
    up_proj = lax.dot_general(x, wu, NT, preferred_element_type=jnp.float32)
    sigmoid = jax.nn.sigmoid(gate_proj)
    activated = gate_proj * sigmoid
    hidden = (activated * up_proj).astype(jnp.bfloat16)
    acc_out[...] += jnp.dot(hidden, wd, preferred_element_type=jnp.float32)
    hidden_grad = lax.dot_general(c, wd, NT, preferred_element_type=jnp.float32)
    gate_grad = (hidden_grad * up_proj * sigmoid * (1.0 + gate_proj * (1.0 - sigmoid))).astype(
        jnp.bfloat16
    )
    up_grad = (hidden_grad * activated).astype(jnp.bfloat16)
    acc_grad[...] += jnp.dot(gate_grad, wg, preferred_element_type=jnp.float32) + jnp.dot(
        up_grad, wu, preferred_element_type=jnp.float32
    )

    @pl.when(step == pl.num_programs(0) - 1)
    def _():
        rows = out_ref.shape[:2]
        out_ref[:, :, :features] = acc_out[...].astype(out_ref.dtype).reshape(rows + (features,))
        out_ref[:, :, features:] = acc_grad[...].astype(out_ref.dtype).reshape(rows + (features,))


def expert_work(rows, w_gate, w_up, w_down, part, parts):
    chunks, cap = rows.shape[:2]
    m = chunks * cap
    hidden_units, features = w_gate.shape
    share = hidden_units // parts
    block = min(512, share)
    steps = share // block
    offset = jnp.reshape(part * steps, (1,)).astype(jnp.int32)
    row_spec = lambda half: pl.BlockSpec((chunks, cap, features), lambda i, off: (0, 0, half))
    w_spec = pl.BlockSpec((block, features), lambda i, off: (off[0] + i, 0))
    out_spec = pl.BlockSpec((chunks, cap, 2 * features), lambda i, off: (0, 0, 0))
    cost = pl.CostEstimate(
        flops=12 * m * share * features,
        transcendentals=m * share,
        bytes_accessed=3 * share * features * 2 + 4 * m * features * 2,
    )
    grid_spec = pltpu.PrefetchScalarGridSpec(
        num_scalar_prefetch=1,
        grid=(steps,),
        in_specs=[row_spec(0), row_spec(1), w_spec, w_spec, w_spec],
        out_specs=out_spec,
        scratch_shapes=[pltpu.VMEM((m, features), jnp.float32)] * 2,
    )
    return pl.pallas_call(
        expert_kernel,
        grid_spec=grid_spec,
        out_shape=jax.ShapeDtypeStruct((chunks, cap, 2 * features), jnp.bfloat16),
        compiler_params=pltpu.CompilerParams(
            dimension_semantics=("arbitrary",), vmem_limit_bytes=48 * 1024 * 1024
        ),
        cost_estimate=cost,
    )(offset, rows, rows, w_gate, w_up, w_down)


def pair_rank(ids_ref, p):
    e = ids_ref[p % 2, p // 2]
    rank = jnp.int32(0)
    for q in range(p):
        rank = rank + (ids_ref[q % 2, q // 2] == e).astype(jnp.int32)
    return e, rank


def pack_kernel(owner_count, ids_ref, gw_ref, tok_ref, cot_ref, out_ref):
    tok_count, features = tok_ref.shape
    out_ref[...] = jnp.zeros_like(out_ref)
    gw = gw_ref[...].astype(jnp.float32)
    for p in range(2 * tok_count):
        e, rank = pair_rank(ids_ref, p)
        t, k = p // 2, p % 2
        tok_row = tok_ref[t:t + 1, :]
        cot_row = (gw[k:k + 1, t:t + 1] * cot_ref[t:t + 1, :].astype(jnp.float32)).astype(out_ref.dtype)
        for j in range(owner_count):
            o = e * owner_count + j
            for r in range(CAP):
                keep = rank == r
                out_ref[o, r:r + 1, :features] = jnp.where(keep, tok_row, out_ref[o, r:r + 1, :features])
                out_ref[o, r:r + 1, features:] = jnp.where(keep, cot_row, out_ref[o, r:r + 1, features:])


def unpack_kernel(owner_count, ids_ref, gw_ref, home_ref, out_ref, grad_ref):
    tok_count, features = out_ref.shape
    gw = gw_ref[...].astype(jnp.float32)
    for t in range(tok_count):
        total_out = jnp.zeros((1, features), jnp.float32)
        total_grad = jnp.zeros((1, features), jnp.float32)
        for k in range(2):
            e, rank = pair_rank(ids_ref, 2 * t + k)
            part_out = jnp.zeros((1, features), jnp.float32)
            part_grad = jnp.zeros((1, features), jnp.float32)
            for j in range(owner_count):
                block = home_ref[e * owner_count + j].astype(jnp.float32)
                row = jnp.where(rank == 0, block[0:1], block[1:2])
                part_out = part_out + row[:, :features]
                part_grad = part_grad + row[:, features:]
            total_out = total_out + gw[k:k + 1, t:t + 1] * part_out
            total_grad = total_grad + part_grad
        out_ref[t:t + 1, :] = total_out.astype(out_ref.dtype)
        grad_ref[t:t + 1, :] = total_grad.astype(grad_ref.dtype)


SMEM_SPEC = pl.BlockSpec(memory_space=pltpu.SMEM)
VMEM_SPEC = pl.BlockSpec(memory_space=pltpu.VMEM)


def pack(tokens, cotangent, expert_ids, gate_weights, devices):
    owner_count = devices // EXPERTS
    features = tokens.shape[1]
    return pl.pallas_call(
        functools.partial(pack_kernel, owner_count),
        in_specs=[SMEM_SPEC, VMEM_SPEC, VMEM_SPEC, VMEM_SPEC],
        out_specs=VMEM_SPEC,
        out_shape=jax.ShapeDtypeStruct((devices, CAP, 2 * features), tokens.dtype),
    )(expert_ids.T, gate_weights.T, tokens, cotangent)


def unpack(home, expert_ids, gate_weights, devices):
    owner_count = devices // EXPERTS
    tok_count = expert_ids.shape[0]
    features = home.shape[2] // 2
    return pl.pallas_call(
        functools.partial(unpack_kernel, owner_count),
        in_specs=[SMEM_SPEC, VMEM_SPEC, VMEM_SPEC],
        out_specs=[VMEM_SPEC, VMEM_SPEC],
        out_shape=[jax.ShapeDtypeStruct((tok_count, features), home.dtype)] * 2,
    )(expert_ids.T, gate_weights.T, home)


def shards(tokens, cotangent, expert_ids, gate_weights, w_gate, w_up, w_down):
    devices = lax.axis_size("expert")
    send = pack(tokens, cotangent, expert_ids, gate_weights, devices)
    recv = lax.all_to_all(send, "expert", split_axis=0, concat_axis=0, tiled=True)
    partials = expert_work(recv, w_gate, w_up, w_down, 0, 1)
    home = lax.all_to_all(partials, "expert", split_axis=0, concat_axis=0, tiled=True)
    layer_out, input_grad = unpack(home, expert_ids, gate_weights, devices)
    return (layer_out, input_grad)


def solution(mesh):
    in_specs = (
        P(("groups", "expert"), None),
        P(("groups", "expert"), None),
        P(("groups", "expert"), None),
        P(("groups", "expert"), None),
        P("expert", None),
        P("expert", None),
        P("expert", None),
    )
    out_specs = (P(("groups", "expert"), None), P(("groups", "expert"), None))
    return jax.shard_map(shards, mesh=mesh, in_specs=in_specs, out_specs=out_specs, check_vma=False)
```

```python
import functools

import jax
import jax.numpy as jnp
from jax import lax
from jax.experimental import pallas as pl
from jax.experimental.pallas import tpu as pltpu
from jax.sharding import PartitionSpec as P

EXPERTS = 8
CAP = 2
NT = (((1,), (1,)), ((), ()))


def slot_ranks(routes):
    count = routes.shape[-1]
    order = jnp.arange(count, dtype=jnp.int32)
    earlier = order[None, :] < order[:, None]
    same = routes[..., :, None] == routes[..., None, :]
    return jnp.sum(jnp.logical_and(same, earlier), axis=-1)


def expert_kernel(offset_ref, x_ref, c_ref, wg_ref, wu_ref, wd_ref, out_ref, acc_out, acc_grad):
    step = pl.program_id(0)
    features = acc_out.shape[1]

    @pl.when(step == 0)
    def _():
        acc_out[...] = jnp.zeros_like(acc_out)
        acc_grad[...] = jnp.zeros_like(acc_grad)

    m = acc_out.shape[0]
    x = x_ref[...].reshape(m, features)
    c = c_ref[...].reshape(m, features)
    wg = wg_ref[...]
    wu = wu_ref[...]
    wd = wd_ref[...]
    gate_proj = lax.dot_general(x, wg, NT, preferred_element_type=jnp.float32)
    up_proj = lax.dot_general(x, wu, NT, preferred_element_type=jnp.float32)
    sigmoid = jax.nn.sigmoid(gate_proj)
    activated = gate_proj * sigmoid
    hidden = (activated * up_proj).astype(jnp.bfloat16)
    acc_out[...] += jnp.dot(hidden, wd, preferred_element_type=jnp.float32)
    hidden_grad = lax.dot_general(c, wd, NT, preferred_element_type=jnp.float32)
    gate_grad = (hidden_grad * up_proj * sigmoid * (1.0 + gate_proj * (1.0 - sigmoid))).astype(
        jnp.bfloat16
    )
    up_grad = (hidden_grad * activated).astype(jnp.bfloat16)
    acc_grad[...] += jnp.dot(gate_grad, wg, preferred_element_type=jnp.float32) + jnp.dot(
        up_grad, wu, preferred_element_type=jnp.float32
    )

    @pl.when(step == pl.num_programs(0) - 1)
    def _():
        rows = out_ref.shape[:2]
        out_ref[:, :, :features] = acc_out[...].astype(out_ref.dtype).reshape(rows + (features,))
        out_ref[:, :, features:] = acc_grad[...].astype(out_ref.dtype).reshape(rows + (features,))


def expert_work(rows, w_gate, w_up, w_down, part, parts):
    chunks, cap = rows.shape[:2]
    m = chunks * cap
    hidden_units, features = w_gate.shape
    share = hidden_units // parts
    block = min(512, share)
    steps = share // block
    offset = jnp.reshape(part * steps, (1,)).astype(jnp.int32)
    row_spec = lambda half: pl.BlockSpec((chunks, cap, features), lambda i, off: (0, 0, half))
    w_spec = pl.BlockSpec((block, features), lambda i, off: (off[0] + i, 0))
    out_spec = pl.BlockSpec((chunks, cap, 2 * features), lambda i, off: (0, 0, 0))
    cost = pl.CostEstimate(
        flops=12 * m * share * features,
        transcendentals=m * share,
        bytes_accessed=3 * share * features * 2 + 4 * m * features * 2,
    )
    grid_spec = pltpu.PrefetchScalarGridSpec(
        num_scalar_prefetch=1,
        grid=(steps,),
        in_specs=[row_spec(0), row_spec(1), w_spec, w_spec, w_spec],
        out_specs=out_spec,
        scratch_shapes=[pltpu.VMEM((m, features), jnp.float32)] * 2,
    )
    return pl.pallas_call(
        expert_kernel,
        grid_spec=grid_spec,
        out_shape=jax.ShapeDtypeStruct((chunks, cap, 2 * features), jnp.bfloat16),
        compiler_params=pltpu.CompilerParams(
            dimension_semantics=("arbitrary",),
            vmem_limit_bytes=48 * 1024 * 1024,
        ),
        cost_estimate=cost,
    )(offset, rows, rows, w_gate, w_up, w_down)


def pair_rank(ids_ref, p):
    e = ids_ref[p % 2, p // 2]
    rank = jnp.int32(0)
    for q in range(p):
        rank = rank + (ids_ref[q % 2, q // 2] == e).astype(jnp.int32)
    return e, rank


def selectors(owner_count, ids_ref, gw_ref, rows, tok_count):
    row = lax.broadcasted_iota(jnp.int32, (rows, tok_count), 0)
    col = lax.broadcasted_iota(jnp.int32, (rows, tok_count), 1)
    gw = gw_ref[...].astype(jnp.float32)
    pick = jnp.zeros((rows, tok_count), jnp.float32)
    weight = jnp.zeros((rows, tok_count), jnp.float32)
    for p in range(2 * tok_count):
        e, rank = pair_rank(ids_ref, p)
        t, k = p // 2, p % 2
        hit = (col == t) & (row // (owner_count * CAP) == e) & (row % CAP == rank)
        pick = jnp.where(hit, 1.0, pick)
        weight = jnp.where(hit, gw[k:k + 1, :], weight)
    return pick, weight


def pack_kernel(owner_count, ids_ref, gw_ref, tok_ref, cot_ref, out_ref):
    tok_count, features = tok_ref.shape
    chunks, cap = out_ref.shape[:2]
    pick, weight = selectors(owner_count, ids_ref, gw_ref, chunks * cap, tok_count)
    send_tok = jnp.dot(pick.astype(tok_ref.dtype), tok_ref[...], preferred_element_type=jnp.float32)
    send_cot = jnp.dot(weight.astype(cot_ref.dtype), cot_ref[...], preferred_element_type=jnp.float32)
    out_ref[:, :, :features] = send_tok.astype(out_ref.dtype).reshape((chunks, cap, features))
    out_ref[:, :, features:] = send_cot.astype(out_ref.dtype).reshape((chunks, cap, features))


def unpack_kernel(owner_count, ids_ref, gw_ref, home_ref, out_ref, grad_ref):
    tok_count, features = out_ref.shape
    chunks, cap = home_ref.shape[:2]
    pick, weight = selectors(owner_count, ids_ref, gw_ref, chunks * cap, tok_count)
    home = home_ref[...].reshape((chunks * cap, 2 * features))
    contract = (((0,), (0,)), ((), ()))
    out = lax.dot_general(weight.astype(home.dtype), home[:, :features], contract, preferred_element_type=jnp.float32)
    grad = lax.dot_general(pick.astype(home.dtype), home[:, features:], contract, preferred_element_type=jnp.float32)
    out_ref[...] = out.astype(out_ref.dtype)
    grad_ref[...] = grad.astype(grad_ref.dtype)


SMEM_SPEC = pl.BlockSpec(memory_space=pltpu.SMEM)
VMEM_SPEC = pl.BlockSpec(memory_space=pltpu.VMEM)


def pack(tokens, cotangent, expert_ids, gate_weights, devices):
    owner_count = devices // EXPERTS
    features = tokens.shape[1]
    return pl.pallas_call(
        functools.partial(pack_kernel, owner_count),
        in_specs=[SMEM_SPEC, VMEM_SPEC, VMEM_SPEC, VMEM_SPEC],
        out_specs=VMEM_SPEC,
        out_shape=jax.ShapeDtypeStruct((devices, CAP, 2 * features), tokens.dtype),
    )(expert_ids.T, gate_weights.T, tokens, cotangent)


def unpack(home, expert_ids, gate_weights, devices):
    owner_count = devices // EXPERTS
    tok_count = expert_ids.shape[0]
    features = home.shape[2] // 2
    return pl.pallas_call(
        functools.partial(unpack_kernel, owner_count),
        in_specs=[SMEM_SPEC, VMEM_SPEC, VMEM_SPEC],
        out_specs=[VMEM_SPEC, VMEM_SPEC],
        out_shape=[jax.ShapeDtypeStruct((tok_count, features), home.dtype)] * 2,
    )(expert_ids.T, gate_weights.T, home)


def shards(tokens, cotangent, expert_ids, gate_weights, w_gate, w_up, w_down):
    devices = lax.axis_size("expert")
    send = pack(tokens, cotangent, expert_ids, gate_weights, devices)
    recv = lax.all_to_all(send, "expert", split_axis=0, concat_axis=0, tiled=True)
    partials = expert_work(recv, w_gate, w_up, w_down, 0, 1)
    home = lax.all_to_all(partials, "expert", split_axis=0, concat_axis=0, tiled=True)
    layer_out, input_grad = unpack(home, expert_ids, gate_weights, devices)
    return (layer_out, input_grad)


def solution(mesh):
    in_specs = (
        P(("groups", "expert"), None),
        P(("groups", "expert"), None),
        P(("groups", "expert"), None),
        P(("groups", "expert"), None),
        P("expert", None),
        P("expert", None),
        P("expert", None),
    )
    out_specs = (P(("groups", "expert"), None), P(("groups", "expert"), None))
    return jax.shard_map(shards, mesh=mesh, in_specs=in_specs, out_specs=out_specs, check_vma=False)
```

```python
import functools

import jax
import jax.numpy as jnp
from jax import lax
from jax.experimental import pallas as pl
from jax.experimental.pallas import tpu as pltpu
from jax.sharding import PartitionSpec as P

EXPERTS = 8
CAP = 2
NT = (((1,), (1,)), ((), ()))


def slot_ranks(routes):
    count = routes.shape[-1]
    order = jnp.arange(count, dtype=jnp.int32)
    earlier = order[None, :] < order[:, None]
    same = routes[..., :, None] == routes[..., None, :]
    return jnp.sum(jnp.logical_and(same, earlier), axis=-1)


def expert_kernel(offset_ref, x_ref, c_ref, wg_ref, wu_ref, wd_ref, out_ref, acc_out, acc_grad):
    step = pl.program_id(0)
    features = acc_out.shape[1]

    @pl.when(step == 0)
    def _():
        acc_out[...] = jnp.zeros_like(acc_out)
        acc_grad[...] = jnp.zeros_like(acc_grad)

    m = acc_out.shape[0]
    x = x_ref[...].reshape(m, features)
    c = c_ref[...].reshape(m, features)
    wg = wg_ref[...]
    wu = wu_ref[...]
    wd = wd_ref[...]
    gate_proj = lax.dot_general(x, wg, NT, preferred_element_type=jnp.float32)
    up_proj = lax.dot_general(x, wu, NT, preferred_element_type=jnp.float32)
    sigmoid = jax.nn.sigmoid(gate_proj)
    activated = gate_proj * sigmoid
    hidden = (activated * up_proj).astype(jnp.bfloat16)
    acc_out[...] += jnp.dot(hidden, wd, preferred_element_type=jnp.float32)
    hidden_grad = lax.dot_general(c, wd, NT, preferred_element_type=jnp.float32)
    gate_grad = (hidden_grad * up_proj * sigmoid * (1.0 + gate_proj * (1.0 - sigmoid))).astype(
        jnp.bfloat16
    )
    up_grad = (hidden_grad * activated).astype(jnp.bfloat16)
    acc_grad[...] += jnp.dot(gate_grad, wg, preferred_element_type=jnp.float32) + jnp.dot(
        up_grad, wu, preferred_element_type=jnp.float32
    )

    @pl.when(step == pl.num_programs(0) - 1)
    def _():
        rows = out_ref.shape[:2]
        out_ref[:, :, :features] = acc_out[...].astype(out_ref.dtype).reshape(rows + (features,))
        out_ref[:, :, features:] = acc_grad[...].astype(out_ref.dtype).reshape(rows + (features,))


def expert_work(rows, w_gate, w_up, w_down, part, parts):
    chunks, cap = rows.shape[:2]
    m = chunks * cap
    hidden_units, features = w_gate.shape
    share = hidden_units // parts
    block = min(512, share)
    steps = share // block
    offset = jnp.reshape(part * steps, (1,)).astype(jnp.int32)
    row_spec = lambda half: pl.BlockSpec((chunks, cap, features), lambda i, off: (0, 0, half))
    w_spec = pl.BlockSpec((block, features), lambda i, off: (off[0] + i, 0))
    out_spec = pl.BlockSpec((chunks, cap, 2 * features), lambda i, off: (0, 0, 0))
    cost = pl.CostEstimate(
        flops=12 * m * share * features,
        transcendentals=m * share,
        bytes_accessed=3 * share * features * 2 + 4 * m * features * 2,
    )
    grid_spec = pltpu.PrefetchScalarGridSpec(
        num_scalar_prefetch=1,
        grid=(steps,),
        in_specs=[row_spec(0), row_spec(1), w_spec, w_spec, w_spec],
        out_specs=out_spec,
        scratch_shapes=[pltpu.VMEM((m, features), jnp.float32)] * 2,
    )
    return pl.pallas_call(
        expert_kernel,
        grid_spec=grid_spec,
        out_shape=jax.ShapeDtypeStruct((chunks, cap, 2 * features), jnp.bfloat16),
        compiler_params=pltpu.CompilerParams(
            dimension_semantics=("arbitrary",),
            vmem_limit_bytes=48 * 1024 * 1024,
        ),
        cost_estimate=cost,
    )(offset, rows, rows, w_gate, w_up, w_down)


def pair_rank(ids_ref, p):
    e = ids_ref[p % 2, p // 2]
    rank = jnp.int32(0)
    for q in range(p):
        rank = rank + (ids_ref[q % 2, q // 2] == e).astype(jnp.int32)
    return e, rank


def selectors(owner_count, ids_ref, gw_ref, rows, tok_count):
    row = lax.broadcasted_iota(jnp.int32, (rows, tok_count), 0)
    col = lax.broadcasted_iota(jnp.int32, (rows, tok_count), 1)
    gw = gw_ref[...].astype(jnp.float32)
    pick = jnp.zeros((rows, tok_count), jnp.float32)
    weight = jnp.zeros((rows, tok_count), jnp.float32)
    for p in range(2 * tok_count):
        e, rank = pair_rank(ids_ref, p)
        t, k = p // 2, p % 2
        hit = (col == t) & (row // (owner_count * CAP) == e) & (row % CAP == rank)
        pick = jnp.where(hit, 1.0, pick)
        weight = jnp.where(hit, gw[k:k + 1, :], weight)
    return pick, weight


def pack_kernel(owner_count, ids_ref, gw_ref, tok_ref, cot_ref, out_ref):
    tok_count, features = tok_ref.shape
    chunks, cap = out_ref.shape[:2]
    pick, weight = selectors(owner_count, ids_ref, gw_ref, chunks * cap, tok_count)
    send_tok = jnp.dot(pick.astype(tok_ref.dtype), tok_ref[...], preferred_element_type=jnp.float32)
    send_cot = jnp.dot(weight.astype(cot_ref.dtype), cot_ref[...], preferred_element_type=jnp.float32)
    out_ref[:, :, :features] = send_tok.astype(out_ref.dtype).reshape((chunks, cap, features))
    out_ref[:, :, features:] = send_cot.astype(out_ref.dtype).reshape((chunks, cap, features))


def unpack_kernel(owner_count, ids_ref, gw_ref, home_ref, out_ref, grad_ref):
    tok_count, features = out_ref.shape
    chunks, cap = home_ref.shape[:2]
    pick, weight = selectors(owner_count, ids_ref, gw_ref, chunks * cap, tok_count)
    home = home_ref[...].reshape((chunks * cap, 2 * features))
    contract = (((0,), (0,)), ((), ()))
    out = lax.dot_general(weight.astype(home.dtype), home[:, :features], contract, preferred_element_type=jnp.float32)
    grad = lax.dot_general(pick.astype(home.dtype), home[:, features:], contract, preferred_element_type=jnp.float32)
    out_ref[...] = out.astype(out_ref.dtype)
    grad_ref[...] = grad.astype(grad_ref.dtype)


SMEM_SPEC = pl.BlockSpec(memory_space=pltpu.SMEM)
GLUE_PARAMS = pltpu.CompilerParams()
VMEM_SPEC = pl.BlockSpec(memory_space=pltpu.VMEM)


def pack(tokens, cotangent, expert_ids, gate_weights, devices):
    owner_count = devices // EXPERTS
    features = tokens.shape[1]
    return pl.pallas_call(
        functools.partial(pack_kernel, owner_count),
        in_specs=[SMEM_SPEC, VMEM_SPEC, VMEM_SPEC, VMEM_SPEC],
        out_specs=VMEM_SPEC,
        out_shape=jax.ShapeDtypeStruct((devices, CAP, 2 * features), tokens.dtype),
        compiler_params=GLUE_PARAMS,
    )(expert_ids.T, gate_weights.T, tokens, cotangent)


def unpack(home, expert_ids, gate_weights, devices):
    owner_count = devices // EXPERTS
    tok_count = expert_ids.shape[0]
    features = home.shape[2] // 2
    return pl.pallas_call(
        functools.partial(unpack_kernel, owner_count),
        in_specs=[SMEM_SPEC, VMEM_SPEC, VMEM_SPEC],
        out_specs=[VMEM_SPEC, VMEM_SPEC],
        out_shape=[jax.ShapeDtypeStruct((tok_count, features), home.dtype)] * 2,
        compiler_params=GLUE_PARAMS,
    )(expert_ids.T, gate_weights.T, home)


def shards(tokens, cotangent, expert_ids, gate_weights, w_gate, w_up, w_down):
    devices = lax.axis_size("expert")
    send = pack(tokens, cotangent, expert_ids, gate_weights, devices)
    recv = lax.all_to_all(send, "expert", split_axis=0, concat_axis=0, tiled=True)
    partials = expert_work(recv, w_gate, w_up, w_down, 0, 1)
    home = lax.all_to_all(partials, "expert", split_axis=0, concat_axis=0, tiled=True)
    layer_out, input_grad = unpack(home, expert_ids, gate_weights, devices)
    return (layer_out, input_grad)


def solution(mesh):
    in_specs = (
        P(("groups", "expert"), None),
        P(("groups", "expert"), None),
        P(("groups", "expert"), None),
        P(("groups", "expert"), None),
        P("expert", None),
        P("expert", None),
        P("expert", None),
    )
    out_specs = (P(("groups", "expert"), None), P(("groups", "expert"), None))
    return jax.shard_map(shards, mesh=mesh, in_specs=in_specs, out_specs=out_specs, check_vma=False)
```

```python
import functools

import jax
import jax.numpy as jnp
from jax import lax
from jax.experimental import pallas as pl
from jax.experimental.pallas import tpu as pltpu
from jax.sharding import PartitionSpec as P

EXPERTS = 8
CAP = 2
NT = (((1,), (1,)), ((), ()))


def slot_ranks(routes):
    count = routes.shape[-1]
    order = jnp.arange(count, dtype=jnp.int32)
    earlier = order[None, :] < order[:, None]
    same = routes[..., :, None] == routes[..., None, :]
    return jnp.sum(jnp.logical_and(same, earlier), axis=-1)


def expert_kernel(x_ref, c_ref, wg_ref, wu_ref, wd_hbm, out_ref, acc_out, acc_grad, wd_buf, sem):
    step = pl.program_id(0)
    steps = pl.num_programs(0)
    features = acc_out.shape[1]
    block = wd_buf.shape[1]
    slot = step % 2

    def wd_copy(i, s):
        rows = pl.ds(pl.multiple_of(i * block, block), block)
        return pltpu.make_async_copy(wd_hbm.at[rows, :], wd_buf.at[s], sem.at[s])

    @pl.when(step == 0)
    def _():
        wd_copy(0, 0).start()
        acc_out[...] = jnp.zeros_like(acc_out)
        acc_grad[...] = jnp.zeros_like(acc_grad)

    @pl.when(step + 1 < steps)
    def _():
        wd_copy(step + 1, 1 - slot).start()

    m = acc_out.shape[0]
    x = x_ref[...].reshape(m, features)
    c = c_ref[...].reshape(m, features)
    wg = wg_ref[...]
    wu = wu_ref[...]
    gate_proj = lax.dot_general(x, wg, NT, preferred_element_type=jnp.float32)
    up_proj = lax.dot_general(x, wu, NT, preferred_element_type=jnp.float32)
    sigmoid = jax.nn.sigmoid(gate_proj)
    activated = gate_proj * sigmoid
    hidden = (activated * up_proj).astype(jnp.bfloat16)
    wd_copy(step, slot).wait()
    wd = wd_buf[slot]
    acc_out[...] += jnp.dot(hidden, wd, preferred_element_type=jnp.float32)
    hidden_grad = lax.dot_general(c, wd, NT, preferred_element_type=jnp.float32)
    gate_grad = (hidden_grad * up_proj * sigmoid * (1.0 + gate_proj * (1.0 - sigmoid))).astype(
        jnp.bfloat16
    )
    up_grad = (hidden_grad * activated).astype(jnp.bfloat16)
    acc_grad[...] += jnp.dot(gate_grad, wg, preferred_element_type=jnp.float32) + jnp.dot(
        up_grad, wu, preferred_element_type=jnp.float32
    )

    @pl.when(step == steps - 1)
    def _():
        rows = out_ref.shape[:2]
        out_ref[:, :, :features] = acc_out[...].astype(out_ref.dtype).reshape(rows + (features,))
        out_ref[:, :, features:] = acc_grad[...].astype(out_ref.dtype).reshape(rows + (features,))


def expert_work(rows, w_gate, w_up, w_down):
    chunks, cap = rows.shape[:2]
    m = chunks * cap
    hidden_units, features = w_gate.shape
    block = min(512, hidden_units)
    steps = hidden_units // block
    row_spec = lambda half: pl.BlockSpec((chunks, cap, features), lambda i: (0, 0, half))
    w_spec = pl.BlockSpec((block, features), lambda i: (i, 0))
    out_spec = pl.BlockSpec((chunks, cap, 2 * features), lambda i: (0, 0, 0))
    cost = pl.CostEstimate(
        flops=12 * m * hidden_units * features,
        transcendentals=m * hidden_units,
        bytes_accessed=3 * hidden_units * features * 2 + 4 * m * features * 2,
    )
    return pl.pallas_call(
        expert_kernel,
        grid=(steps,),
        in_specs=[row_spec(0), row_spec(1), w_spec, w_spec, pl.BlockSpec(memory_space=pl.ANY)],
        out_specs=out_spec,
        out_shape=jax.ShapeDtypeStruct((chunks, cap, 2 * features), jnp.bfloat16),
        scratch_shapes=[
            pltpu.VMEM((m, features), jnp.float32),
            pltpu.VMEM((m, features), jnp.float32),
            pltpu.VMEM((2, block, features), w_down.dtype),
            pltpu.SemaphoreType.DMA((2,)),
        ],
        compiler_params=pltpu.CompilerParams(
            dimension_semantics=("arbitrary",),
            vmem_limit_bytes=48 * 1024 * 1024,
        ),
        cost_estimate=cost,
    )(rows, rows, w_gate, w_up, w_down)


def pair_rank(ids_ref, p):
    e = ids_ref[p % 2, p // 2]
    rank = jnp.int32(0)
    for q in range(p):
        rank = rank + (ids_ref[q % 2, q // 2] == e).astype(jnp.int32)
    return e, rank


def selectors(owner_count, ids_ref, gw_ref, rows, tok_count):
    row = lax.broadcasted_iota(jnp.int32, (rows, tok_count), 0)
    col = lax.broadcasted_iota(jnp.int32, (rows, tok_count), 1)
    gw = gw_ref[...].astype(jnp.float32)
    pick = jnp.zeros((rows, tok_count), jnp.float32)
    weight = jnp.zeros((rows, tok_count), jnp.float32)
    for p in range(2 * tok_count):
        e, rank = pair_rank(ids_ref, p)
        t, k = p // 2, p % 2
        hit = (col == t) & (row // (owner_count * CAP) == e) & (row % CAP == rank)
        pick = jnp.where(hit, 1.0, pick)
        weight = jnp.where(hit, gw[k:k + 1, :], weight)
    return pick, weight


def pack_kernel(owner_count, ids_ref, gw_ref, tok_ref, cot_ref, out_ref):
    tok_count, features = tok_ref.shape
    chunks, cap = out_ref.shape[:2]
    pick, weight = selectors(owner_count, ids_ref, gw_ref, chunks * cap, tok_count)
    send_tok = jnp.dot(pick.astype(tok_ref.dtype), tok_ref[...], preferred_element_type=jnp.float32)
    send_cot = jnp.dot(weight.astype(cot_ref.dtype), cot_ref[...], preferred_element_type=jnp.float32)
    out_ref[:, :, :features] = send_tok.astype(out_ref.dtype).reshape((chunks, cap, features))
    out_ref[:, :, features:] = send_cot.astype(out_ref.dtype).reshape((chunks, cap, features))


def unpack_kernel(owner_count, ids_ref, gw_ref, home_ref, out_ref, grad_ref):
    tok_count, features = out_ref.shape
    chunks, cap = home_ref.shape[:2]
    pick, weight = selectors(owner_count, ids_ref, gw_ref, chunks * cap, tok_count)
    home = home_ref[...].reshape((chunks * cap, 2 * features))
    contract = (((0,), (0,)), ((), ()))
    out = lax.dot_general(weight.astype(home.dtype), home[:, :features], contract, preferred_element_type=jnp.float32)
    grad = lax.dot_general(pick.astype(home.dtype), home[:, features:], contract, preferred_element_type=jnp.float32)
    out_ref[...] = out.astype(out_ref.dtype)
    grad_ref[...] = grad.astype(grad_ref.dtype)


SMEM_SPEC = pl.BlockSpec(memory_space=pltpu.SMEM)
VMEM_SPEC = pl.BlockSpec(memory_space=pltpu.VMEM)


def pack(tokens, cotangent, expert_ids, gate_weights, devices):
    owner_count = devices // EXPERTS
    features = tokens.shape[1]
    return pl.pallas_call(
        functools.partial(pack_kernel, owner_count),
        in_specs=[SMEM_SPEC, VMEM_SPEC, VMEM_SPEC, VMEM_SPEC],
        out_specs=VMEM_SPEC,
        out_shape=jax.ShapeDtypeStruct((devices, CAP, 2 * features), tokens.dtype),
    )(expert_ids.T, gate_weights.T, tokens, cotangent)


def unpack(home, expert_ids, gate_weights, devices):
    owner_count = devices // EXPERTS
    tok_count = expert_ids.shape[0]
    features = home.shape[2] // 2
    return pl.pallas_call(
        functools.partial(unpack_kernel, owner_count),
        in_specs=[SMEM_SPEC, VMEM_SPEC, VMEM_SPEC],
        out_specs=[VMEM_SPEC, VMEM_SPEC],
        out_shape=[jax.ShapeDtypeStruct((tok_count, features), home.dtype)] * 2,
    )(expert_ids.T, gate_weights.T, home)


def shards(tokens, cotangent, expert_ids, gate_weights, w_gate, w_up, w_down):
    devices = lax.axis_size("expert")
    send = pack(tokens, cotangent, expert_ids, gate_weights, devices)
    recv = lax.all_to_all(send, "expert", split_axis=0, concat_axis=0, tiled=True)
    partials = expert_work(recv, w_gate, w_up, w_down)
    home = lax.all_to_all(partials, "expert", split_axis=0, concat_axis=0, tiled=True)
    layer_out, input_grad = unpack(home, expert_ids, gate_weights, devices)
    return (layer_out, input_grad)


def solution(mesh):
    in_specs = (
        P(("groups", "expert"), None),
        P(("groups", "expert"), None),
        P(("groups", "expert"), None),
        P(("groups", "expert"), None),
        P("expert", None),
        P("expert", None),
        P("expert", None),
    )
    out_specs = (P(("groups", "expert"), None), P(("groups", "expert"), None))
    return jax.shard_map(shards, mesh=mesh, in_specs=in_specs, out_specs=out_specs, check_vma=False)
```

```python
import functools

import jax
import jax.numpy as jnp
from jax import lax
from jax.experimental import pallas as pl
from jax.experimental.pallas import tpu as pltpu
from jax.sharding import PartitionSpec as P

EXPERTS = 8
CAP = 2
NT = (((1,), (1,)), ((), ()))


def slot_ranks(routes):
    count = routes.shape[-1]
    order = jnp.arange(count, dtype=jnp.int32)
    earlier = order[None, :] < order[:, None]
    same = routes[..., :, None] == routes[..., None, :]
    return jnp.sum(jnp.logical_and(same, earlier), axis=-1)


def expert_kernel(offset_ref, x_ref, c_ref, wg_ref, wu_ref, wd_ref, out_ref, acc_out, acc_grad):
    step = pl.program_id(0)
    features = acc_out.shape[1]

    @pl.when(step == 0)
    def _():
        acc_out[...] = jnp.zeros_like(acc_out)
        acc_grad[...] = jnp.zeros_like(acc_grad)

    m = acc_out.shape[0]
    x = x_ref[...].reshape(m, features)
    c = c_ref[...].reshape(m, features)
    wg = wg_ref[...]
    wu = wu_ref[...]
    wd = wd_ref[...]
    gate_proj = lax.dot_general(x, wg, NT, preferred_element_type=jnp.float32)
    up_proj = lax.dot_general(x, wu, NT, preferred_element_type=jnp.float32)
    sigmoid = jax.nn.sigmoid(gate_proj)
    activated = gate_proj * sigmoid
    hidden = (activated * up_proj).astype(jnp.bfloat16)
    acc_out[...] += jnp.dot(hidden, wd, preferred_element_type=jnp.float32)
    hidden_grad = lax.dot_general(c, wd, NT, preferred_element_type=jnp.float32)
    gate_grad = (hidden_grad * up_proj * sigmoid * (1.0 + gate_proj * (1.0 - sigmoid))).astype(
        jnp.bfloat16
    )
    up_grad = (hidden_grad * activated).astype(jnp.bfloat16)
    acc_grad[...] += jnp.dot(gate_grad, wg, preferred_element_type=jnp.float32) + jnp.dot(
        up_grad, wu, preferred_element_type=jnp.float32
    )

    @pl.when(step == pl.num_programs(0) - 1)
    def _():
        rows = out_ref.shape[:2]
        out_ref[:, :, :features] = acc_out[...].astype(out_ref.dtype).reshape(rows + (features,))
        out_ref[:, :, features:] = acc_grad[...].astype(out_ref.dtype).reshape(rows + (features,))


def expert_work(rows, w_gate, w_up, w_down, part, parts):
    chunks, cap = rows.shape[:2]
    m = chunks * cap
    hidden_units, features = w_gate.shape
    share = hidden_units // parts
    block = min(512, share)
    steps = share // block
    offset = jnp.reshape(part * steps, (1,)).astype(jnp.int32)
    row_spec = lambda half: pl.BlockSpec((chunks, cap, features), lambda i, off: (0, 0, half))
    w_spec = pl.BlockSpec((block, features), lambda i, off: (off[0] + i, 0))
    out_spec = pl.BlockSpec((chunks, cap, 2 * features), lambda i, off: (0, 0, 0))
    cost = pl.CostEstimate(
        flops=12 * m * share * features,
        transcendentals=m * share,
        bytes_accessed=3 * share * features * 2 + 4 * m * features * 2,
    )
    grid_spec = pltpu.PrefetchScalarGridSpec(
        num_scalar_prefetch=1,
        grid=(steps,),
        in_specs=[row_spec(0), row_spec(1), w_spec, w_spec, w_spec],
        out_specs=out_spec,
        scratch_shapes=[pltpu.VMEM((m, features), jnp.float32)] * 2,
    )
    return pl.pallas_call(
        expert_kernel,
        grid_spec=grid_spec,
        out_shape=jax.ShapeDtypeStruct((chunks, cap, 2 * features), jnp.bfloat16),
        compiler_params=pltpu.CompilerParams(
            dimension_semantics=("arbitrary",),
            vmem_limit_bytes=48 * 1024 * 1024,
        ),
        cost_estimate=cost,
    )(offset, rows, rows, w_gate, w_up, w_down)


def pair_rank(ids_ref, p):
    e = ids_ref[p % 2, p // 2]
    rank = jnp.int32(0)
    for q in range(p):
        rank = rank + (ids_ref[q % 2, q // 2] == e).astype(jnp.int32)
    return e, rank


def selectors(owner_count, ids_ref, gw_ref, rows, tok_count):
    row = lax.broadcasted_iota(jnp.int32, (rows, tok_count), 0)
    col = lax.broadcasted_iota(jnp.int32, (rows, tok_count), 1)
    gw = gw_ref[...].astype(jnp.float32)
    pick = jnp.zeros((rows, tok_count), jnp.float32)
    weight = jnp.zeros((rows, tok_count), jnp.float32)
    for p in range(2 * tok_count):
        e, rank = pair_rank(ids_ref, p)
        t, k = p // 2, p % 2
        hit = (col == t) & (row // (owner_count * CAP) == e) & (row % CAP == rank)
        pick = jnp.where(hit, 1.0, pick)
        weight = jnp.where(hit, gw[k:k + 1, :], weight)
    return pick, weight


def pack_kernel(owner_count, ids_ref, gw_ref, tok_ref, cot_ref, out_ref, pick_ref, weight_ref):
    tok_count, features = tok_ref.shape
    chunks, cap = out_ref.shape[:2]
    pick, weight = selectors(owner_count, ids_ref, gw_ref, chunks * cap, tok_count)
    pick_ref[...] = pick
    weight_ref[...] = weight
    send_tok = jnp.dot(pick.astype(tok_ref.dtype), tok_ref[...], preferred_element_type=jnp.float32)
    send_cot = jnp.dot(weight.astype(cot_ref.dtype), cot_ref[...], preferred_element_type=jnp.float32)
    out_ref[:, :, :features] = send_tok.astype(out_ref.dtype).reshape((chunks, cap, features))
    out_ref[:, :, features:] = send_cot.astype(out_ref.dtype).reshape((chunks, cap, features))


def unpack_kernel(pick_ref, weight_ref, home_ref, out_ref, grad_ref):
    tok_count, features = out_ref.shape
    chunks, cap = home_ref.shape[:2]
    pick = pick_ref[...]
    weight = weight_ref[...]
    home = home_ref[...].reshape((chunks * cap, 2 * features))
    contract = (((0,), (0,)), ((), ()))
    out = lax.dot_general(weight.astype(home.dtype), home[:, :features], contract, preferred_element_type=jnp.float32)
    grad = lax.dot_general(pick.astype(home.dtype), home[:, features:], contract, preferred_element_type=jnp.float32)
    out_ref[...] = out.astype(out_ref.dtype)
    grad_ref[...] = grad.astype(grad_ref.dtype)


SMEM_SPEC = pl.BlockSpec(memory_space=pltpu.SMEM)
VMEM_SPEC = pl.BlockSpec(memory_space=pltpu.VMEM)


def pack(tokens, cotangent, expert_ids, gate_weights, devices):
    owner_count = devices // EXPERTS
    tok_count, features = tokens.shape
    select = jax.ShapeDtypeStruct((devices * CAP, tok_count), jnp.float32)
    return pl.pallas_call(
        functools.partial(pack_kernel, owner_count),
        in_specs=[SMEM_SPEC, VMEM_SPEC, VMEM_SPEC, VMEM_SPEC],
        out_specs=[VMEM_SPEC, VMEM_SPEC, VMEM_SPEC],
        out_shape=[jax.ShapeDtypeStruct((devices, CAP, 2 * features), tokens.dtype), select, select],
    )(expert_ids.T, gate_weights.T, tokens, cotangent)


def unpack(home, pick, weight):
    tok_count = pick.shape[1]
    features = home.shape[2] // 2
    return pl.pallas_call(
        unpack_kernel,
        in_specs=[VMEM_SPEC, VMEM_SPEC, VMEM_SPEC],
        out_specs=[VMEM_SPEC, VMEM_SPEC],
        out_shape=[jax.ShapeDtypeStruct((tok_count, features), home.dtype)] * 2,
    )(pick, weight, home)


def shards(tokens, cotangent, expert_ids, gate_weights, w_gate, w_up, w_down):
    devices = lax.axis_size("expert")
    send, pick, weight = pack(tokens, cotangent, expert_ids, gate_weights, devices)
    recv = lax.all_to_all(send, "expert", split_axis=0, concat_axis=0, tiled=True)
    partials = expert_work(recv, w_gate, w_up, w_down, 0, 1)
    home = lax.all_to_all(partials, "expert", split_axis=0, concat_axis=0, tiled=True)
    layer_out, input_grad = unpack(home, pick, weight)
    return (layer_out, input_grad)


def solution(mesh):
    in_specs = (
        P(("groups", "expert"), None),
        P(("groups", "expert"), None),
        P(("groups", "expert"), None),
        P(("groups", "expert"), None),
        P("expert", None),
        P("expert", None),
        P("expert", None),
    )
    out_specs = (P(("groups", "expert"), None), P(("groups", "expert"), None))
    return jax.shard_map(shards, mesh=mesh, in_specs=in_specs, out_specs=out_specs, check_vma=False)
```

```python
import functools

import jax
import jax.numpy as jnp
from jax import lax
from jax.experimental import pallas as pl
from jax.experimental.pallas import tpu as pltpu
from jax.sharding import PartitionSpec as P

EXPERTS = 8
CAP = 2
NT = (((1,), (1,)), ((), ()))


def slot_ranks(routes):
    count = routes.shape[-1]
    order = jnp.arange(count, dtype=jnp.int32)
    earlier = order[None, :] < order[:, None]
    same = routes[..., :, None] == routes[..., None, :]
    return jnp.sum(jnp.logical_and(same, earlier), axis=-1)


def expert_kernel(
    offset_ref, x_ref, c_ref, wg_ref, wu_ref, wd_ref, out_ref, acc_out, acc_grad, x_rows, c_rows
):
    step = pl.program_id(0)
    m, features = acc_out.shape

    @pl.when(step == 0)
    def _():
        acc_out[...] = jnp.zeros_like(acc_out)
        acc_grad[...] = jnp.zeros_like(acc_grad)
        x_rows[...] = x_ref[...].reshape(m, features)
        c_rows[...] = c_ref[...].reshape(m, features)

    x = x_rows[...]
    c = c_rows[...]
    wg = wg_ref[...]
    wu = wu_ref[...]
    wd = wd_ref[...]
    gate_proj = lax.dot_general(x, wg, NT, preferred_element_type=jnp.float32)
    up_proj = lax.dot_general(x, wu, NT, preferred_element_type=jnp.float32)
    sigmoid = jax.nn.sigmoid(gate_proj)
    activated = gate_proj * sigmoid
    hidden = (activated * up_proj).astype(jnp.bfloat16)
    acc_out[...] += jnp.dot(hidden, wd, preferred_element_type=jnp.float32)
    hidden_grad = lax.dot_general(c, wd, NT, preferred_element_type=jnp.float32)
    gate_grad = (hidden_grad * up_proj * sigmoid * (1.0 + gate_proj * (1.0 - sigmoid))).astype(
        jnp.bfloat16
    )
    up_grad = (hidden_grad * activated).astype(jnp.bfloat16)
    acc_grad[...] += jnp.dot(gate_grad, wg, preferred_element_type=jnp.float32) + jnp.dot(
        up_grad, wu, preferred_element_type=jnp.float32
    )

    @pl.when(step == pl.num_programs(0) - 1)
    def _():
        rows = out_ref.shape[:2]
        out_ref[:, :, :features] = acc_out[...].astype(out_ref.dtype).reshape(rows + (features,))
        out_ref[:, :, features:] = acc_grad[...].astype(out_ref.dtype).reshape(rows + (features,))


def expert_work(rows, w_gate, w_up, w_down, part, parts):
    chunks, cap = rows.shape[:2]
    m = chunks * cap
    hidden_units, features = w_gate.shape
    share = hidden_units // parts
    block = min(512, share)
    steps = share // block
    offset = jnp.reshape(part * steps, (1,)).astype(jnp.int32)
    row_spec = lambda half: pl.BlockSpec((chunks, cap, features), lambda i, off: (0, 0, half))
    w_spec = pl.BlockSpec((block, features), lambda i, off: (off[0] + i, 0))
    out_spec = pl.BlockSpec((chunks, cap, 2 * features), lambda i, off: (0, 0, 0))
    cost = pl.CostEstimate(
        flops=12 * m * share * features,
        transcendentals=m * share,
        bytes_accessed=3 * share * features * 2 + 4 * m * features * 2,
    )
    grid_spec = pltpu.PrefetchScalarGridSpec(
        num_scalar_prefetch=1,
        grid=(steps,),
        in_specs=[row_spec(0), row_spec(1), w_spec, w_spec, w_spec],
        out_specs=out_spec,
        scratch_shapes=[pltpu.VMEM((m, features), jnp.float32)] * 2
        + [pltpu.VMEM((m, features), rows.dtype)] * 2,
    )
    return pl.pallas_call(
        expert_kernel,
        grid_spec=grid_spec,
        out_shape=jax.ShapeDtypeStruct((chunks, cap, 2 * features), jnp.bfloat16),
        compiler_params=pltpu.CompilerParams(
            dimension_semantics=("arbitrary",),
            vmem_limit_bytes=48 * 1024 * 1024,
        ),
        cost_estimate=cost,
    )(offset, rows, rows, w_gate, w_up, w_down)


def pair_rank(ids_ref, p):
    e = ids_ref[p % 2, p // 2]
    rank = jnp.int32(0)
    for q in range(p):
        rank = rank + (ids_ref[q % 2, q // 2] == e).astype(jnp.int32)
    return e, rank


def selectors(owner_count, ids_ref, gw_ref, rows, tok_count):
    row = lax.broadcasted_iota(jnp.int32, (rows, tok_count), 0)
    col = lax.broadcasted_iota(jnp.int32, (rows, tok_count), 1)
    gw = gw_ref[...].astype(jnp.float32)
    pick = jnp.zeros((rows, tok_count), jnp.float32)
    weight = jnp.zeros((rows, tok_count), jnp.float32)
    for p in range(2 * tok_count):
        e, rank = pair_rank(ids_ref, p)
        t, k = p // 2, p % 2
        hit = (col == t) & (row // (owner_count * CAP) == e) & (row % CAP == rank)
        pick = jnp.where(hit, 1.0, pick)
        weight = jnp.where(hit, gw[k:k + 1, :], weight)
    return pick, weight


def pack_kernel(owner_count, ids_ref, gw_ref, tok_ref, cot_ref, out_ref, pick_ref, weight_ref):
    tok_count, features = tok_ref.shape
    chunks, cap = out_ref.shape[:2]
    pick, weight = selectors(owner_count, ids_ref, gw_ref, chunks * cap, tok_count)
    pick_ref[...] = pick
    weight_ref[...] = weight
    send_tok = jnp.dot(pick.astype(tok_ref.dtype), tok_ref[...], preferred_element_type=jnp.float32)
    send_cot = jnp.dot(weight.astype(cot_ref.dtype), cot_ref[...], preferred_element_type=jnp.float32)
    out_ref[:, :, :features] = send_tok.astype(out_ref.dtype).reshape((chunks, cap, features))
    out_ref[:, :, features:] = send_cot.astype(out_ref.dtype).reshape((chunks, cap, features))


def unpack_kernel(pick_ref, weight_ref, home_ref, out_ref, grad_ref):
    tok_count, features = out_ref.shape
    chunks, cap = home_ref.shape[:2]
    pick = pick_ref[...]
    weight = weight_ref[...]
    home = home_ref[...].reshape((chunks * cap, 2 * features))
    contract = (((0,), (0,)), ((), ()))
    out = lax.dot_general(weight.astype(home.dtype), home[:, :features], contract, preferred_element_type=jnp.float32)
    grad = lax.dot_general(pick.astype(home.dtype), home[:, features:], contract, preferred_element_type=jnp.float32)
    out_ref[...] = out.astype(out_ref.dtype)
    grad_ref[...] = grad.astype(grad_ref.dtype)


SMEM_SPEC = pl.BlockSpec(memory_space=pltpu.SMEM)
VMEM_SPEC = pl.BlockSpec(memory_space=pltpu.VMEM)


def pack(tokens, cotangent, expert_ids, gate_weights, devices):
    owner_count = devices // EXPERTS
    tok_count, features = tokens.shape
    select = jax.ShapeDtypeStruct((devices * CAP, tok_count), jnp.float32)
    return pl.pallas_call(
        functools.partial(pack_kernel, owner_count),
        in_specs=[SMEM_SPEC, VMEM_SPEC, VMEM_SPEC, VMEM_SPEC],
        out_specs=[VMEM_SPEC, VMEM_SPEC, VMEM_SPEC],
        out_shape=[jax.ShapeDtypeStruct((devices, CAP, 2 * features), tokens.dtype), select, select],
    )(expert_ids.T, gate_weights.T, tokens, cotangent)


def unpack(home, pick, weight):
    tok_count = pick.shape[1]
    features = home.shape[2] // 2
    return pl.pallas_call(
        unpack_kernel,
        in_specs=[VMEM_SPEC, VMEM_SPEC, VMEM_SPEC],
        out_specs=[VMEM_SPEC, VMEM_SPEC],
        out_shape=[jax.ShapeDtypeStruct((tok_count, features), home.dtype)] * 2,
    )(pick, weight, home)


def shards(tokens, cotangent, expert_ids, gate_weights, w_gate, w_up, w_down):
    devices = lax.axis_size("expert")
    send, pick, weight = pack(tokens, cotangent, expert_ids, gate_weights, devices)
    recv = lax.all_to_all(send, "expert", split_axis=0, concat_axis=0, tiled=True)
    partials = expert_work(recv, w_gate, w_up, w_down, 0, 1)
    home = lax.all_to_all(partials, "expert", split_axis=0, concat_axis=0, tiled=True)
    layer_out, input_grad = unpack(home, pick, weight)
    return (layer_out, input_grad)


def solution(mesh):
    in_specs = (
        P(("groups", "expert"), None),
        P(("groups", "expert"), None),
        P(("groups", "expert"), None),
        P(("groups", "expert"), None),
        P("expert", None),
        P("expert", None),
        P("expert", None),
    )
    out_specs = (P(("groups", "expert"), None), P(("groups", "expert"), None))
    return jax.shard_map(shards, mesh=mesh, in_specs=in_specs, out_specs=out_specs, check_vma=False)
```

```python
import functools

import jax
import jax.numpy as jnp
from jax import lax
from jax.experimental import pallas as pl
from jax.experimental.pallas import tpu as pltpu
from jax.sharding import PartitionSpec as P

EXPERTS = 8
CAP = 2
NT = (((1,), (1,)), ((), ()))


def slot_ranks(routes):
    count = routes.shape[-1]
    order = jnp.arange(count, dtype=jnp.int32)
    earlier = order[None, :] < order[:, None]
    same = routes[..., :, None] == routes[..., None, :]
    return jnp.sum(jnp.logical_and(same, earlier), axis=-1)


def expert_kernel(offset_ref, x_ref, c_ref, wg_ref, wu_ref, wd_ref, out_ref, acc_out, acc_grad):
    step = pl.program_id(0)
    features = acc_out.shape[1]

    @pl.when(step == 0)
    def _():
        acc_out[...] = jnp.zeros_like(acc_out)
        acc_grad[...] = jnp.zeros_like(acc_grad)

    m = acc_out.shape[0]
    x = x_ref[...].reshape(m, features)
    c = c_ref[...].reshape(m, features)
    wg = wg_ref[...]
    wu = wu_ref[...]
    wd = wd_ref[...]
    gate_proj = lax.dot_general(x, wg, NT, preferred_element_type=jnp.float32)
    up_proj = lax.dot_general(x, wu, NT, preferred_element_type=jnp.float32)
    sigmoid = jax.nn.sigmoid(gate_proj)
    activated = gate_proj * sigmoid
    hidden = (activated * up_proj).astype(jnp.bfloat16)
    acc_out[...] += jnp.dot(hidden, wd, preferred_element_type=jnp.float32)
    hidden_grad = lax.dot_general(c, wd, NT, preferred_element_type=jnp.float32)
    gate_grad = (hidden_grad * up_proj * sigmoid * (1.0 + gate_proj * (1.0 - sigmoid))).astype(
        jnp.bfloat16
    )
    up_grad = (hidden_grad * activated).astype(jnp.bfloat16)
    acc_grad[...] += jnp.dot(gate_grad, wg, preferred_element_type=jnp.float32) + jnp.dot(
        up_grad, wu, preferred_element_type=jnp.float32
    )

    @pl.when(step == pl.num_programs(0) - 1)
    def _():
        rows = out_ref.shape[:2]
        out_ref[:, :, :features] = acc_out[...].astype(out_ref.dtype).reshape(rows + (features,))
        out_ref[:, :, features:] = acc_grad[...].astype(out_ref.dtype).reshape(rows + (features,))


def expert_work(rows, w_gate, w_up, w_down, part, parts):
    chunks, cap = rows.shape[:2]
    m = chunks * cap
    hidden_units, features = w_gate.shape
    share = hidden_units // parts
    block = min(512, share)
    steps = share // block
    offset = jnp.reshape(part * steps, (1,)).astype(jnp.int32)
    row_spec = lambda half: pl.BlockSpec((chunks, cap, features), lambda i, off: (0, 0, half))
    w_spec = pl.BlockSpec((block, features), lambda i, off: (off[0] + i, 0))
    out_spec = pl.BlockSpec((chunks, cap, 2 * features), lambda i, off: (0, 0, 0))
    cost = pl.CostEstimate(
        flops=12 * m * share * features,
        transcendentals=m * share,
        bytes_accessed=3 * share * features * 2 + 4 * m * features * 2,
    )
    grid_spec = pltpu.PrefetchScalarGridSpec(
        num_scalar_prefetch=1,
        grid=(steps,),
        in_specs=[row_spec(0), row_spec(1), w_spec, w_spec, w_spec],
        out_specs=out_spec,
        scratch_shapes=[pltpu.VMEM((m, features), jnp.float32)] * 2,
    )
    return pl.pallas_call(
        expert_kernel,
        grid_spec=grid_spec,
        out_shape=jax.ShapeDtypeStruct((chunks, cap, 2 * features), jnp.bfloat16),
        compiler_params=pltpu.CompilerParams(
            dimension_semantics=("arbitrary",),
            vmem_limit_bytes=48 * 1024 * 1024,
        ),
        cost_estimate=cost,
    )(offset, rows, rows, w_gate, w_up, w_down)


def pair_rank(ids_ref, p):
    e = ids_ref[p % 2, p // 2]
    rank = jnp.int32(0)
    for q in range(p):
        rank = rank + (ids_ref[q % 2, q // 2] == e).astype(jnp.int32)
    return e, rank


def selectors(owner_count, ids_ref, gw_ref, rows, tok_count):
    row = lax.broadcasted_iota(jnp.int32, (rows, tok_count), 0)
    col = lax.broadcasted_iota(jnp.int32, (rows, tok_count), 1)
    gw = gw_ref[...].astype(jnp.float32)
    pick = jnp.zeros((rows, tok_count), jnp.float32)
    weight = jnp.zeros((rows, tok_count), jnp.float32)
    for p in range(2 * tok_count):
        e, rank = pair_rank(ids_ref, p)
        t, k = p // 2, p % 2
        hit = (col == t) & (row // (owner_count * CAP) == e) & (row % CAP == rank)
        pick = jnp.where(hit, 1.0, pick)
        weight = jnp.where(hit, gw[k:k + 1, :], weight)
    return pick, weight


def pack_kernel(owner_count, ids_ref, gw_ref, tok_ref, cot_ref, out_ref, pick_ref, weight_ref):
    tok_count, features = tok_ref.shape
    chunks, cap = out_ref.shape[:2]
    pick, weight = selectors(owner_count, ids_ref, gw_ref, chunks * cap, tok_count)
    pick_ref[...] = pick.astype(pick_ref.dtype)
    weight_ref[...] = weight.astype(weight_ref.dtype)
    send_tok = jnp.dot(pick.astype(tok_ref.dtype), tok_ref[...], preferred_element_type=jnp.float32)
    send_cot = jnp.dot(weight.astype(cot_ref.dtype), cot_ref[...], preferred_element_type=jnp.float32)
    out_ref[:, :, :features] = send_tok.astype(out_ref.dtype).reshape((chunks, cap, features))
    out_ref[:, :, features:] = send_cot.astype(out_ref.dtype).reshape((chunks, cap, features))


def unpack_kernel(pick_ref, weight_ref, home_ref, out_ref, grad_ref):
    tok_count, features = out_ref.shape
    chunks, cap = home_ref.shape[:2]
    pick = pick_ref[...]
    weight = weight_ref[...]
    home = home_ref[...].reshape((chunks * cap, 2 * features))
    contract = (((0,), (0,)), ((), ()))
    out = lax.dot_general(weight.astype(home.dtype), home[:, :features], contract, preferred_element_type=jnp.float32)
    grad = lax.dot_general(pick.astype(home.dtype), home[:, features:], contract, preferred_element_type=jnp.float32)
    out_ref[...] = out.astype(out_ref.dtype)
    grad_ref[...] = grad.astype(grad_ref.dtype)


SMEM_SPEC = pl.BlockSpec(memory_space=pltpu.SMEM)
VMEM_SPEC = pl.BlockSpec(memory_space=pltpu.VMEM)


def pack(tokens, cotangent, expert_ids, gate_weights, devices):
    owner_count = devices // EXPERTS
    tok_count, features = tokens.shape
    select = jax.ShapeDtypeStruct((devices * CAP, tok_count), tokens.dtype)
    return pl.pallas_call(
        functools.partial(pack_kernel, owner_count),
        in_specs=[SMEM_SPEC, VMEM_SPEC, VMEM_SPEC, VMEM_SPEC],
        out_specs=[VMEM_SPEC, VMEM_SPEC, VMEM_SPEC],
        out_shape=[jax.ShapeDtypeStruct((devices, CAP, 2 * features), tokens.dtype), select, select],
    )(expert_ids.T, gate_weights.T, tokens, cotangent)


def unpack(home, pick, weight):
    tok_count = pick.shape[1]
    features = home.shape[2] // 2
    return pl.pallas_call(
        unpack_kernel,
        in_specs=[VMEM_SPEC, VMEM_SPEC, VMEM_SPEC],
        out_specs=[VMEM_SPEC, VMEM_SPEC],
        out_shape=[jax.ShapeDtypeStruct((tok_count, features), home.dtype)] * 2,
    )(pick, weight, home)


def shards(tokens, cotangent, expert_ids, gate_weights, w_gate, w_up, w_down):
    devices = lax.axis_size("expert")
    send, pick, weight = pack(tokens, cotangent, expert_ids, gate_weights, devices)
    recv = lax.all_to_all(send, "expert", split_axis=0, concat_axis=0, tiled=True)
    partials = expert_work(recv, w_gate, w_up, w_down, 0, 1)
    home = lax.all_to_all(partials, "expert", split_axis=0, concat_axis=0, tiled=True)
    layer_out, input_grad = unpack(home, pick, weight)
    return (layer_out, input_grad)


def solution(mesh):
    in_specs = (
        P(("groups", "expert"), None),
        P(("groups", "expert"), None),
        P(("groups", "expert"), None),
        P(("groups", "expert"), None),
        P("expert", None),
        P("expert", None),
        P("expert", None),
    )
    out_specs = (P(("groups", "expert"), None), P(("groups", "expert"), None))
    return jax.shard_map(shards, mesh=mesh, in_specs=in_specs, out_specs=out_specs, check_vma=False)
```
